32 devices in a mesh: row: 8 (over y, x, core), col: 4 (over z).
Axes of the slice: x: 2, y: 2, z: 4, core: 2. Of those that a mesh axis runs over, the one named last changes fastest.
Arguments:
- magnetic_potential_input: bfloat16 [32, 32768], P('row', 'col'), may hold values from -6 to 6
- node_reordering: int32 [32768], P('col'), may hold values from 0 to 32767, as said below
- adjacent_dense_blocks: bfloat16 [512, 256, 256], P(('row', 'col')), may hold values from -0.375 to 0.375
- adjacent_cluster_pairs: int32 [512, 2], P(('row', 'col')), may hold values from 0 to 127, as said below
- distant_row_factors: bfloat16 [960, 256, 32], P(('row', 'col')), may hold values from -1 to 1
- distant_row_factor_index: int32 [960, 2], P(('row', 'col')), may hold values from 0 to 127, as said below
- distant_column_factors: bfloat16 [960, 256, 32], P(('row', 'col')), may hold values from -0.125 to 0.125
- distant_column_factor_index: int32 [960, 2], P(('row', 'col')), may hold values from 0 to 127, as said below
Outputs:
- field: float32 [32, 32768], P('col', 'row')
The draws below stay inside these ranges and needn't reach their ends.
Inputs may be any that keep to these rules, and one draw needn't show every extreme that they name: `node_reordering`: each column block of positions k * 32 * 256 to (k + 1) * 32 * 256 - 1 is mapped one to one onto the initial nodes of the same range. `adjacent_cluster_pairs`: slot of device d with row index i: the row cluster lies in i * 16 to (i + 1) * 16 - 1; the column cluster lies within 3 of the row cluster and in column block h = i * (col devices) // (row devices), clusters h * 32 to (h + 1) * 32 - 1. `distant_row_factor_index`: piece of device d with row index i: column 0 is a leaf cluster in i * 16 to (i + 1) * 16 - 1; column 1 is a block slot 0 to 7. A block of level l has 2**l row pieces on 2**l aligned consecutive clusters; each level 0 to 3 has 2 blocks a device. `distant_column_factor_index`: piece of device d with col index j: column 0 is a leaf cluster in j * 32 to (j + 1) * 32 - 1; column 1 is a block slot as in distant_row_factor_index; a block has as many column pieces as row pieces, on aligned consecutive clusters.
All inputs are finite; a program needn't handle non-finite values.
Results may differ from the reference program's by a relative error of at most 0.0023.
Values may be sent and summed in bfloat16 or wider, within the bound.
No kernel may reach another device: no remote copies, remote signals or barrier semaphores. Data moves between devices by JAX's collectives and lax.ppermute only.
A program may use at most 64 MiB of HBM per device.

```python
import jax
import jax.numpy as jnp
import numpy as np
from jax import lax

LEAF = 256
RANK = 32
STATES = 32
RC = 16
NEAR_DEV = 16
BL = 2
NODES = 32768
CB = 32
NEAR = 512
FARP = 960
N_ROW = 8
N_COL = 4


def draw_node_reordering(key, part):
    width = CB * LEAF
    groups = NODES // width
    keys = jax.random.split(key, groups)
    orders = jax.vmap(lambda k: jax.random.permutation(k, width))(keys)
    offsets = (jnp.arange(groups, dtype=jnp.int32) * width)[:, None]
    return (orders.astype(jnp.int32) + offsets).reshape(NODES)


def draw_adjacent_cluster_pairs(key, part):
    col_count = NODES // (CB * LEAF)
    row_count = NODES // (RC * LEAF)
    slots = jnp.arange(NEAR, dtype=jnp.int32)
    device = slots // NEAR_DEV
    row_index = device // col_count
    home = row_index * col_count // row_count
    first = jax.random.randint(jax.random.fold_in(key, 1), (NEAR,), 0, RC, dtype=jnp.int32)
    offset = jax.random.randint(jax.random.fold_in(key, 2), (NEAR,), -3, 4, dtype=jnp.int32)
    row_cluster = row_index * RC + first
    col_cluster = jnp.clip(row_cluster + offset, home * CB, home * CB + CB - 1)
    return jnp.stack([row_cluster, col_cluster], axis=-1).astype(jnp.int32)


def far_pieces(key, side):
    col_count = NODES // (CB * LEAF)
    processor_units = FARP // (15 * BL)
    factor_fragments = 15 * BL
    block_entries = 4 * BL
    block_list = []
    offset_list = []
    level_of_block = []
    for level in range(4):
        for item in range(BL):
            level_of_block.append(level)
            for step in range(2 ** level):
                block_list.append(level * BL + item)
                offset_list.append(step)
    block_table = jnp.asarray(np.array(block_list, dtype=np.int32))
    offset_table = jnp.asarray(np.array(offset_list, dtype=np.int32))
    size_table = jnp.asarray(np.array([2 ** v for v in level_of_block], dtype=np.int32))
    relabel = jax.vmap(lambda k: jax.random.permutation(k, block_entries))(jax.random.split(jax.random.fold_in(key, 11), processor_units)).astype(jnp.int32)
    device = jnp.arange(processor_units, dtype=jnp.int32)
    if side == 0:
        cluster_extent = RC
        base = device // col_count * RC
    else:
        cluster_extent = CB
        base = device % col_count * CB
    raw = jax.random.randint(jax.random.fold_in(key, 20 + side), (processor_units, block_entries), 0, 2 ** 30, dtype=jnp.int32)
    start = raw % (cluster_extent // size_table)[None, :] * size_table[None, :]
    leaf = base[:, None] + start[:, block_table] + offset_table[None, :]
    label = relabel[:, block_table]
    order = jax.vmap(lambda k: jax.random.permutation(k, factor_fragments))(jax.random.split(jax.random.fold_in(key, 30 + side), processor_units)).astype(jnp.int32)
    leaf = jnp.take_along_axis(leaf, order, axis=1)
    label = jnp.take_along_axis(label, order, axis=1)
    return jnp.stack([leaf, label], axis=-1).reshape(FARP, 2).astype(jnp.int32)


def draw_distant_row_factor_index(key, part):
    return far_pieces(key, 0)


def draw_distant_column_factor_index(key, part):
    return far_pieces(key, 1)


def shard_levels(key, dims, pieces, low, high):
    factor_of, own = 1.0, jax.random.fold_in(key, 6)
    for position, shards_of in pieces:
        heights = jnp.exp(jax.random.uniform(jax.random.fold_in(own, position), (shards_of,), jnp.float32, low / len(pieces), high / len(pieces)))
        factor_of = factor_of * jnp.repeat(heights, dims[position] // shards_of).reshape([-1 if axis == position else 1 for axis in range(len(dims))])
    return factor_of


def normal_values(rng, extent, scale, bound, cuts=(), held_as=jnp.bfloat16):
    drawn = jax.random.normal(rng, extent, jnp.float32) * scale
    if len(cuts) > 0:
        drawn = shard_levels(rng, extent, cuts, -0.22, 0.18) * drawn
    return jnp.clip(drawn, min=-bound, max=bound).astype(held_as)


def setup_inputs(seed: int = 0) -> dict:
    key_list = jax.random.split(jax.random.key(seed), 9)
    magnetic_potential_input = normal_values(key_list[0], (STATES, NODES), 1.0, 6.0, ((0, 8), (1, 4)))
    node_reordering = draw_node_reordering(jax.random.fold_in(key_list[8], 71), 0)
    adjacent_dense_blocks = normal_values(key_list[2], (NEAR, LEAF, LEAF), LEAF ** -0.5, 0.375, ((0, 32),))
    adjacent_cluster_pairs = draw_adjacent_cluster_pairs(jax.random.fold_in(key_list[8], 71), 0)
    distant_row_factors = normal_values(key_list[4], (FARP, LEAF, RANK), RANK ** -0.5, 1.0, ((0, 32),))
    distant_row_factor_index = draw_distant_row_factor_index(jax.random.fold_in(key_list[8], 71), 0)
    distant_column_factors = normal_values(key_list[6], (FARP, LEAF, RANK), (8 * LEAF) ** -0.5, 0.125, ((0, 32),))
    distant_column_factor_index = draw_distant_column_factor_index(jax.random.fold_in(key_list[8], 71), 0)
    return dict(magnetic_potential_input=magnetic_potential_input, node_reordering=node_reordering, adjacent_dense_blocks=adjacent_dense_blocks, adjacent_cluster_pairs=adjacent_cluster_pairs, distant_row_factors=distant_row_factors, distant_row_factor_index=distant_row_factor_index, distant_column_factors=distant_column_factors, distant_column_factor_index=distant_column_factor_index)


def reference(magnetic_potential_input, node_reordering, adjacent_dense_blocks, adjacent_cluster_pairs, distant_row_factors, distant_row_factor_index, distant_column_factors, distant_column_factor_index):
    processor_units = N_ROW * N_COL
    block_entries = 4 * BL
    factor_fragments = 15 * BL
    clusters = RC * N_ROW
    ordered = jnp.take(magnetic_potential_input, node_reordering, axis=0 + 1)
    leaf_clusters = ordered.reshape(STATES, clusters, LEAF).transpose(1, 0, 2)

    def device_step(field, items):
        mats, pairs, u_mats, u_index, v_mats, v_index = items
        near_src = leaf_clusters[pairs[:, 1]].astype(jnp.float32)
        near_out = jnp.einsum('nsk,nlk->nsl', near_src, mats.astype(jnp.float32))
        field = field.at[pairs[:, 0]].add(near_out)
        distant_source_values = leaf_clusters[v_index[:, 0]].astype(jnp.float32)
        coeffs = jnp.einsum('psk,pkr->prs', distant_source_values, v_mats.astype(jnp.float32))
        summed = jax.ops.segment_sum(coeffs, v_index[:, 1], num_segments=block_entries)
        rounded = lax.optimization_barrier(summed.astype(jnp.bfloat16)).astype(jnp.float32)
        picked = rounded[u_index[:, 1]]
        far_out = jnp.einsum('prs,plr->psl', picked, u_mats.astype(jnp.float32))
        field = field.at[u_index[:, 0]].add(far_out)
        return field, None

    field = jnp.zeros((clusters, STATES, LEAF), jnp.float32)
    items = (adjacent_dense_blocks.reshape(processor_units, NEAR_DEV, LEAF, LEAF),
             adjacent_cluster_pairs.reshape(processor_units, NEAR_DEV, 2),
             distant_row_factors.reshape(processor_units, factor_fragments, LEAF, RANK),
             distant_row_factor_index.reshape(processor_units, factor_fragments, 2),
             distant_column_factors.reshape(processor_units, factor_fragments, LEAF, RANK),
             distant_column_factor_index.reshape(processor_units, factor_fragments, 2))
    field, _ = lax.scan(device_step, field, items)
    return field.transpose(1, 0, 2).reshape(STATES, clusters * LEAF)
```

```python
import jax
import jax.numpy as jnp
from jax import lax
from jax.sharding import PartitionSpec as P

BL = 2
REACH = 3


def per_device(
    magnetic_potential_input,
    node_reordering,
    adjacent_dense_blocks,
    adjacent_cluster_pairs,
    distant_row_factors,
    distant_row_factor_index,
    distant_column_factors,
    distant_column_factor_index,
):
    row_count = lax.axis_size("row")
    col_count = lax.axis_size("col")
    row_index = lax.axis_index("row")
    col_index = lax.axis_index("col")
    local_states, width = magnetic_potential_input.shape
    states = local_states * row_count
    leaf = adjacent_dense_blocks.shape[1]
    rank = distant_row_factors.shape[2]
    cluster_extent = width // leaf
    row_span = cluster_extent * col_count // row_count
    window = 0
    for target in range(row_count):
        base_t = target * row_span - target * col_count // row_count * cluster_extent
        low_t = max(base_t - REACH, 0)
        high_t = min(base_t + row_span + REACH, cluster_extent)
        window = max(window, high_t - low_t)
    block_entries = 4 * BL

    local_order = node_reordering - col_index * width
    mine = jnp.take(magnetic_potential_input, local_order, axis=1)

    ordered = lax.all_gather(mine, "row", axis=0, tiled=True)
    leaf_clusters = ordered.reshape(states, cluster_extent, leaf)

    every_block = lax.all_gather(mine, "col", axis=0, tiled=False)
    pieces = []
    for target in range(row_count):
        home_t = target * col_count // row_count
        start_t = min(max(target * row_span - home_t * cluster_extent - REACH, 0), cluster_extent - window)
        pieces.append(every_block[home_t, :, start_t * leaf:(start_t + window) * leaf])
    send = jnp.concatenate(pieces, axis=0)
    near_window = lax.all_to_all(send, "row", 0, 0, tiled=True).reshape(states, window, leaf)

    home = row_index * col_count // row_count
    start = jnp.clip(row_index * row_span - home * cluster_extent - REACH, 0, cluster_extent - window)
    near_cols = adjacent_cluster_pairs[:, 1] - home * cluster_extent - start
    near_rows = adjacent_cluster_pairs[:, 0] - row_index * row_span
    near_src = jnp.take(near_window, near_cols, axis=1)
    near_out = jnp.einsum(
        "snk,nlk->nsl", near_src, adjacent_dense_blocks, preferred_element_type=jnp.float32
    )

    v_src = jnp.take(leaf_clusters, distant_column_factor_index[:, 0] - col_index * cluster_extent, axis=1)
    coeffs = jnp.einsum(
        "spk,pkr->psr", v_src, distant_column_factors, preferred_element_type=jnp.float32
    )
    fragments = coeffs.shape[0]
    column_indicator = (
        distant_column_factor_index[:, 1][None, :]
        == jnp.arange(block_entries, dtype=jnp.int32)[:, None]
    ).astype(jnp.float32)
    summed = jnp.dot(
        column_indicator,
        coeffs.reshape(fragments, states * rank),
        precision=lax.Precision.HIGHEST,
    ).astype(jnp.bfloat16).reshape(block_entries, states, rank)
    picked = jnp.take(summed, distant_row_factor_index[:, 1], axis=0)
    far_out = jnp.einsum(
        "psr,plr->psl", picked, distant_row_factors, preferred_element_type=jnp.float32
    )

    all_out = jnp.concatenate([near_out, far_out], axis=0)
    all_rows = jnp.concatenate([near_rows, distant_row_factor_index[:, 0] - row_index * row_span])
    scatter = (
        all_rows[None, :] == jnp.arange(row_span, dtype=jnp.int32)[:, None]
    ).astype(jnp.float32)
    partial_sum = jnp.dot(
        scatter,
        all_out.reshape(all_out.shape[0], states * leaf),
        precision=lax.Precision.HIGHEST,
    ).reshape(row_span, states, leaf)
    partial_sum = partial_sum.transpose(1, 0, 2).reshape(states, row_span * leaf)
    return lax.psum_scatter(partial_sum, "col", scatter_dimension=0, tiled=True)


def solution(mesh):
    placed = (
        P("row", "col"),
        P("col"),
        P(("row", "col"), None, None),
        P(("row", "col"), None),
        P(("row", "col"), None, None),
        P(("row", "col"), None),
        P(("row", "col"), None, None),
        P(("row", "col"), None),
    )
    return jax.shard_map(
        per_device, mesh=mesh, in_specs=placed, out_specs=P("col", "row"), check_vma=False
    )
```

```python
import jax
import jax.numpy as jnp
from jax import lax
from jax.experimental import pallas as pl
from jax.experimental.pallas import tpu as pltpu
from jax.sharding import PartitionSpec as P

BL = 2
REACH = 3
UNROLL = 16


def _row_gather_kernel(order_ref, rows_ref, out_ref):
    def body(p, carry):
        out_ref[pl.ds(p, 1), :] = rows_ref[pl.ds(order_ref[p], 1), :]
        return carry

    lax.fori_loop(0, out_ref.shape[0], body, 0, unroll=UNROLL)


def reorder(values, order):
    rows = values.astype(jnp.float32).T
    out = pl.pallas_call(
        _row_gather_kernel,
        out_shape=jax.ShapeDtypeStruct(rows.shape, jnp.float32),
        in_specs=[pl.BlockSpec(memory_space=pltpu.SMEM), pl.BlockSpec(memory_space=pltpu.VMEM)],
        out_specs=pl.BlockSpec(memory_space=pltpu.VMEM),
    )(order, rows)
    return out.T.astype(values.dtype)


def per_device(
    magnetic_potential_input,
    node_reordering,
    adjacent_dense_blocks,
    adjacent_cluster_pairs,
    distant_row_factors,
    distant_row_factor_index,
    distant_column_factors,
    distant_column_factor_index,
):
    row_count = lax.axis_size("row")
    col_count = lax.axis_size("col")
    row_index = lax.axis_index("row")
    col_index = lax.axis_index("col")
    local_states, width = magnetic_potential_input.shape
    states = local_states * row_count
    leaf = adjacent_dense_blocks.shape[1]
    rank = distant_row_factors.shape[2]
    cluster_extent = width // leaf
    row_span = cluster_extent * col_count // row_count
    rows_per_home = row_count // col_count
    window = 0
    for target in range(row_count):
        base_t = target * row_span - target * col_count // row_count * cluster_extent
        low_t = max(base_t - REACH, 0)
        high_t = min(base_t + row_span + REACH, cluster_extent)
        window = max(window, high_t - low_t)
    block_entries = 4 * BL

    def window_start(target):
        home_t = target // rows_per_home
        return jnp.clip(target * row_span - home_t * cluster_extent - REACH, 0, cluster_extent - window)

    mine = reorder(magnetic_potential_input, node_reordering - col_index * width)

    chunks = []
    for step in range(row_count):
        slot = (row_index + step) % row_count
        target_row = col_index * rows_per_home + slot // col_count
        piece = lax.dynamic_slice_in_dim(mine, window_start(target_row) * leaf, window * leaf, axis=1)
        pairs = []
        for i in range(row_count):
            for h in range(col_count):
                m = (i + step) % row_count
                pairs.append((i * col_count + h, (h * rows_per_home + m // col_count) * col_count + m % col_count))
        chunks.append(lax.ppermute(piece, ("row", "col"), pairs))

    shards = [mine]
    for step in range(1, row_count):
        shards.append(lax.ppermute(mine, "row", [(i, (i + step) % row_count) for i in range(row_count)]))
    stacked = jnp.stack(shards)
    source_rows = (row_index - jnp.arange(row_count, dtype=jnp.int32)) % row_count
    ordered = jnp.take(stacked, (row_index - jnp.arange(row_count, dtype=jnp.int32)) % row_count, axis=0)
    leaf_clusters = ordered.reshape(states, cluster_extent, leaf)

    home = row_index // rows_per_home
    my_slot = (row_index % rows_per_home) * col_count + col_index
    near_stack = jnp.stack(chunks)
    near_window = jnp.take(
        near_stack, (my_slot - jnp.arange(row_count, dtype=jnp.int32)) % row_count, axis=0
    ).reshape(states, window, leaf)

    near_cols = adjacent_cluster_pairs[:, 1] - home * cluster_extent - window_start(row_index)
    near_rows = adjacent_cluster_pairs[:, 0] - row_index * row_span
    near_src = jnp.take(near_window, near_cols, axis=1)
    near_out = jnp.einsum(
        "snk,nlk->nsl", near_src, adjacent_dense_blocks, preferred_element_type=jnp.float32
    )

    v_src = jnp.take(leaf_clusters, distant_column_factor_index[:, 0] - col_index * cluster_extent, axis=1)
    coeffs = jnp.einsum(
        "spk,pkr->psr", v_src, distant_column_factors, preferred_element_type=jnp.float32
    )
    fragments = coeffs.shape[0]
    column_indicator = (
        distant_column_factor_index[:, 1][None, :]
        == jnp.arange(block_entries, dtype=jnp.int32)[:, None]
    ).astype(jnp.float32)
    summed = jnp.dot(
        column_indicator,
        coeffs.reshape(fragments, states * rank),
        precision=lax.Precision.HIGHEST,
    ).astype(jnp.bfloat16).reshape(block_entries, states, rank)
    picked = jnp.take(summed, distant_row_factor_index[:, 1], axis=0)
    far_out = jnp.einsum(
        "psr,plr->psl", picked, distant_row_factors, preferred_element_type=jnp.float32
    )

    all_out = jnp.concatenate([near_out, far_out], axis=0)
    all_rows = jnp.concatenate([near_rows, distant_row_factor_index[:, 0] - row_index * row_span])
    scatter = (
        all_rows[None, :] == jnp.arange(row_span, dtype=jnp.int32)[:, None]
    ).astype(jnp.float32)
    partial_sum = jnp.dot(
        scatter,
        all_out.reshape(all_out.shape[0], states * leaf),
        precision=lax.Precision.HIGHEST,
    ).reshape(row_span, states, leaf)
    partial_sum = partial_sum.transpose(1, 0, 2).reshape(states, row_span * leaf)

    out_states = states // col_count
    parts = partial_sum.reshape(col_count, out_states, row_span * leaf)
    total = lax.dynamic_index_in_dim(parts, col_index, axis=0, keepdims=False)
    for step in range(1, col_count):
        dest = (col_index + step) % col_count
        piece = lax.dynamic_index_in_dim(parts, dest, axis=0, keepdims=False)
        total = total + lax.ppermute(piece, "col", [(j, (j + step) % col_count) for j in range(col_count)])
    return total


def solution(mesh):
    placed = (
        P("row", "col"),
        P("col"),
        P(("row", "col"), None, None),
        P(("row", "col"), None),
        P(("row", "col"), None, None),
        P(("row", "col"), None),
        P(("row", "col"), None, None),
        P(("row", "col"), None),
    )
    return jax.shard_map(
        per_device, mesh=mesh, in_specs=placed, out_specs=P("col", "row"), check_vma=False
    )
```

```python
import jax
import jax.numpy as jnp
from jax import lax
from jax.experimental import pallas as pl
from jax.sharding import PartitionSpec as P

BL = 2
REACH = 3
LANES = 128
SUBLANES = 8
BATCH = 16


def _lane_gather_kernel(values_ref, low_ref, high_ref, out_ref):
    tiles = values_ref.shape[1] // LANES
    batch = min(BATCH, out_ref.shape[0])

    def group_body(k, carry):
        base = k * batch
        lows = [low_ref[base + b] for b in range(batch)]
        highs = [high_ref[base + b] for b in range(batch)]

        def tile_body(v, accs):
            src = values_ref[:, pl.ds(pl.multiple_of(v * LANES, LANES), LANES)]
            return tuple(
                jnp.where(
                    highs[b] == v,
                    jnp.take_along_axis(src, lows[b], axis=1, mode="promise_in_bounds"),
                    accs[b],
                )
                for b in range(batch)
            )

        zeros = tuple(jnp.zeros((SUBLANES, LANES), jnp.float32) for _ in range(batch))
        accs = lax.fori_loop(0, tiles, tile_body, zeros)
        for b in range(batch):
            out_ref[base + b] = accs[b]
        return carry

    lax.fori_loop(0, out_ref.shape[0] // batch, group_body, 0)


def reorder(values, order):
    rows, width = values.shape
    group = SUBLANES // rows
    groups = width // (LANES * group)
    doubled = jnp.tile(values.astype(jnp.float32), (group, 1))
    index = order.reshape(groups, group, 1, LANES)
    index = jnp.broadcast_to(index, (groups, group, rows, LANES)).reshape(groups, SUBLANES, LANES)
    out = pl.pallas_call(
        _lane_gather_kernel,
        out_shape=jax.ShapeDtypeStruct((groups, SUBLANES, LANES), jnp.float32),
    )(doubled, index % LANES, index // LANES)
    out = out.reshape(groups, group, rows, LANES).transpose(2, 0, 1, 3).reshape(rows, width)
    return out.astype(values.dtype)


def per_device(
    magnetic_potential_input,
    node_reordering,
    adjacent_dense_blocks,
    adjacent_cluster_pairs,
    distant_row_factors,
    distant_row_factor_index,
    distant_column_factors,
    distant_column_factor_index,
):
    row_count = lax.axis_size("row")
    col_count = lax.axis_size("col")
    row_index = lax.axis_index("row")
    col_index = lax.axis_index("col")
    local_states, width = magnetic_potential_input.shape
    states = local_states * row_count
    leaf = adjacent_dense_blocks.shape[1]
    rank = distant_row_factors.shape[2]
    cluster_extent = width // leaf
    row_span = cluster_extent * col_count // row_count
    window = 0
    for target in range(row_count):
        base_t = target * row_span - target * col_count // row_count * cluster_extent
        low_t = max(base_t - REACH, 0)
        high_t = min(base_t + row_span + REACH, cluster_extent)
        window = max(window, high_t - low_t)
    block_entries = 4 * BL

    mine = reorder(magnetic_potential_input, node_reordering - col_index * width)

    ordered = lax.all_gather(mine, "row", axis=0, tiled=True)
    leaf_clusters = ordered.reshape(states, cluster_extent, leaf)

    every_block = lax.all_gather(mine, "col", axis=0, tiled=False)
    pieces = []
    for target in range(row_count):
        home_t = target * col_count // row_count
        start_t = min(max(target * row_span - home_t * cluster_extent - REACH, 0), cluster_extent - window)
        pieces.append(every_block[home_t, :, start_t * leaf:(start_t + window) * leaf])
    send = jnp.concatenate(pieces, axis=0)
    near_window = lax.all_to_all(send, "row", 0, 0, tiled=True).reshape(states, window, leaf)

    home = row_index * col_count // row_count
    start = jnp.clip(row_index * row_span - home * cluster_extent - REACH, 0, cluster_extent - window)
    near_cols = adjacent_cluster_pairs[:, 1] - home * cluster_extent - start
    near_rows = adjacent_cluster_pairs[:, 0] - row_index * row_span
    near_src = jnp.take(near_window, near_cols, axis=1)
    near_out = jnp.einsum(
        "snk,nlk->nsl", near_src, adjacent_dense_blocks, preferred_element_type=jnp.float32
    )

    v_src = jnp.take(leaf_clusters, distant_column_factor_index[:, 0] - col_index * cluster_extent, axis=1)
    coeffs = jnp.einsum(
        "spk,pkr->psr", v_src, distant_column_factors, preferred_element_type=jnp.float32
    )
    fragments = coeffs.shape[0]
    column_indicator = (
        distant_column_factor_index[:, 1][None, :]
        == jnp.arange(block_entries, dtype=jnp.int32)[:, None]
    ).astype(jnp.float32)
    summed = jnp.dot(
        column_indicator,
        coeffs.reshape(fragments, states * rank),
        precision=lax.Precision.HIGHEST,
    ).astype(jnp.bfloat16).reshape(block_entries, states, rank)
    picked = jnp.take(summed, distant_row_factor_index[:, 1], axis=0)
    far_out = jnp.einsum(
        "psr,plr->psl", picked, distant_row_factors, preferred_element_type=jnp.float32
    )

    all_out = jnp.concatenate([near_out, far_out], axis=0)
    all_rows = jnp.concatenate([near_rows, distant_row_factor_index[:, 0] - row_index * row_span])
    scatter = (
        all_rows[None, :] == jnp.arange(row_span, dtype=jnp.int32)[:, None]
    ).astype(jnp.float32)
    partial_sum = jnp.dot(
        scatter,
        all_out.reshape(all_out.shape[0], states * leaf),
        precision=lax.Precision.HIGHEST,
    ).reshape(row_span, states, leaf)
    partial_sum = partial_sum.transpose(1, 0, 2).reshape(states, row_span * leaf)

    exchanged = lax.all_to_all(partial_sum, "col", 0, 0, tiled=True)
    return exchanged.reshape(col_count, states // col_count, row_span * leaf).sum(axis=0)


def solution(mesh):
    placed = (
        P("row", "col"),
        P("col"),
        P(("row", "col"), None, None),
        P(("row", "col"), None),
        P(("row", "col"), None, None),
        P(("row", "col"), None),
        P(("row", "col"), None, None),
        P(("row", "col"), None),
    )
    return jax.shard_map(
        per_device, mesh=mesh, in_specs=placed, out_specs=P("col", "row"), check_vma=False
    )
```

```python
import jax
import jax.numpy as jnp
from jax import lax
from jax.experimental import pallas as pl
from jax.sharding import PartitionSpec as P

BL = 2
REACH = 3
LANES = 128
SUBLANES = 8
BATCH = 16


def _lane_gather_kernel(values_ref, low_ref, high_ref, out_ref):
    tiles = values_ref.shape[1] // LANES
    batch = min(BATCH, out_ref.shape[0])

    def group_body(k, carry):
        base = k * batch
        lows = [low_ref[base + b] for b in range(batch)]
        highs = [high_ref[base + b] for b in range(batch)]

        def tile_body(v, accs):
            src = values_ref[:, pl.ds(pl.multiple_of(v * LANES, LANES), LANES)]
            return tuple(
                jnp.where(
                    highs[b] == v,
                    jnp.take_along_axis(src, lows[b], axis=1, mode="promise_in_bounds"),
                    accs[b],
                )
                for b in range(batch)
            )

        zeros = tuple(jnp.zeros((SUBLANES, LANES), jnp.float32) for _ in range(batch))
        accs = lax.fori_loop(0, tiles, tile_body, zeros)
        for b in range(batch):
            out_ref[base + b] = accs[b]
        return carry

    lax.fori_loop(0, out_ref.shape[0] // batch, group_body, 0)


def reorder(values, order):
    rows, width = values.shape
    group = SUBLANES // rows
    groups = width // (LANES * group)
    doubled = jnp.tile(values.astype(jnp.float32), (group, 1))
    index = order.reshape(groups, group, 1, LANES)
    index = jnp.broadcast_to(index, (groups, group, rows, LANES)).reshape(groups, SUBLANES, LANES)
    out = pl.pallas_call(
        _lane_gather_kernel,
        out_shape=jax.ShapeDtypeStruct((groups, SUBLANES, LANES), jnp.float32),
    )(doubled, index % LANES, index // LANES)
    out = out.reshape(groups, group, rows, LANES).transpose(2, 0, 1, 3).reshape(rows, width)
    return out.astype(values.dtype)


def per_device(
    magnetic_potential_input,
    node_reordering,
    adjacent_dense_blocks,
    adjacent_cluster_pairs,
    distant_row_factors,
    distant_row_factor_index,
    distant_column_factors,
    distant_column_factor_index,
):
    row_count = lax.axis_size("row")
    col_count = lax.axis_size("col")
    row_index = lax.axis_index("row")
    col_index = lax.axis_index("col")
    local_states, width = magnetic_potential_input.shape
    states = local_states * row_count
    leaf = adjacent_dense_blocks.shape[1]
    rank = distant_row_factors.shape[2]
    cluster_extent = width // leaf
    row_span = cluster_extent * col_count // row_count
    window = 0
    for target in range(row_count):
        base_t = target * row_span - target * col_count // row_count * cluster_extent
        low_t = max(base_t - REACH, 0)
        high_t = min(base_t + row_span + REACH, cluster_extent)
        window = max(window, high_t - low_t)
    block_entries = 4 * BL

    mine = reorder(magnetic_potential_input, node_reordering - col_index * width)

    ordered = lax.all_gather(mine, "row", axis=0, tiled=True)
    leaf_clusters = ordered.reshape(states, cluster_extent, leaf)

    every_block = lax.all_to_all(jnp.tile(mine, (col_count, 1)), "col", 0, 0, tiled=True).reshape(
        col_count, local_states, width
    )
    pieces = []
    for target in range(row_count):
        home_t = target * col_count // row_count
        start_t = min(max(target * row_span - home_t * cluster_extent - REACH, 0), cluster_extent - window)
        pieces.append(every_block[home_t, :, start_t * leaf:(start_t + window) * leaf])
    send = jnp.concatenate(pieces, axis=0)
    near_window = lax.all_to_all(send, "row", 0, 0, tiled=True).reshape(states, window, leaf)

    home = row_index * col_count // row_count
    start = jnp.clip(row_index * row_span - home * cluster_extent - REACH, 0, cluster_extent - window)
    near_cols = adjacent_cluster_pairs[:, 1] - home * cluster_extent - start
    near_rows = adjacent_cluster_pairs[:, 0] - row_index * row_span
    near_src = jnp.take(near_window, near_cols, axis=1)
    near_out = jnp.einsum(
        "snk,nlk->nsl", near_src, adjacent_dense_blocks, preferred_element_type=jnp.float32
    )

    v_src = jnp.take(leaf_clusters, distant_column_factor_index[:, 0] - col_index * cluster_extent, axis=1)
    coeffs = jnp.einsum(
        "spk,pkr->psr", v_src, distant_column_factors, preferred_element_type=jnp.float32
    )
    fragments = coeffs.shape[0]
    column_indicator = (
        distant_column_factor_index[:, 1][None, :]
        == jnp.arange(block_entries, dtype=jnp.int32)[:, None]
    ).astype(jnp.float32)
    summed = jnp.dot(
        column_indicator,
        coeffs.reshape(fragments, states * rank),
        precision=lax.Precision.HIGHEST,
    ).astype(jnp.bfloat16).reshape(block_entries, states, rank)
    picked = jnp.take(summed, distant_row_factor_index[:, 1], axis=0)
    far_out = jnp.einsum(
        "psr,plr->psl", picked, distant_row_factors, preferred_element_type=jnp.float32
    )

    all_out = jnp.concatenate([near_out, far_out], axis=0)
    all_rows = jnp.concatenate([near_rows, distant_row_factor_index[:, 0] - row_index * row_span])
    scatter = (
        all_rows[None, :] == jnp.arange(row_span, dtype=jnp.int32)[:, None]
    ).astype(jnp.float32)
    partial_sum = jnp.dot(
        scatter,
        all_out.reshape(all_out.shape[0], states * leaf),
        precision=lax.Precision.HIGHEST,
    ).reshape(row_span, states, leaf)
    partial_sum = partial_sum.transpose(1, 0, 2).reshape(states, row_span * leaf)

    exchanged = lax.all_to_all(partial_sum, "col", 0, 0, tiled=True)
    return exchanged.reshape(col_count, states // col_count, row_span * leaf).sum(axis=0)


def solution(mesh):
    placed = (
        P("row", "col"),
        P("col"),
        P(("row", "col"), None, None),
        P(("row", "col"), None),
        P(("row", "col"), None, None),
        P(("row", "col"), None),
        P(("row", "col"), None, None),
        P(("row", "col"), None),
    )
    return jax.shard_map(
        per_device, mesh=mesh, in_specs=placed, out_specs=P("col", "row"), check_vma=False
    )
```

```python
import jax
import jax.numpy as jnp
from jax import lax
from jax.experimental import pallas as pl
from jax.sharding import PartitionSpec as P

BL = 2
REACH = 3
LANES = 128
SUBLANES = 8
BATCH = 16


def _lane_gather_kernel(values_ref, low_ref, high_ref, out_ref):
    tiles = values_ref.shape[1] // LANES
    batch = min(BATCH, out_ref.shape[0])

    def group_body(k, carry):
        base = k * batch
        lows = [low_ref[base + b] for b in range(batch)]
        highs = [high_ref[base + b] for b in range(batch)]

        def tile_body(v, accs):
            src = values_ref[:, pl.ds(pl.multiple_of(v * LANES, LANES), LANES)]
            return tuple(
                jnp.where(
                    highs[b] == v,
                    jnp.take_along_axis(src, lows[b], axis=1, mode="promise_in_bounds"),
                    accs[b],
                )
                for b in range(batch)
            )

        zeros = tuple(jnp.zeros((SUBLANES, LANES), jnp.float32) for _ in range(batch))
        accs = lax.fori_loop(0, tiles, tile_body, zeros)
        for b in range(batch):
            out_ref[base + b] = accs[b]
        return carry

    lax.fori_loop(0, out_ref.shape[0] // batch, group_body, 0)


def reorder(values, order):
    rows, width = values.shape
    group = SUBLANES // rows
    groups = width // (LANES * group)
    doubled = jnp.tile(values.astype(jnp.float32), (group, 1))
    index = order.reshape(groups, group, 1, LANES)
    index = jnp.broadcast_to(index, (groups, group, rows, LANES)).reshape(groups, SUBLANES, LANES)
    out = pl.pallas_call(
        _lane_gather_kernel,
        out_shape=jax.ShapeDtypeStruct((groups, SUBLANES, LANES), jnp.float32),
    )(doubled, index % LANES, index // LANES)
    out = out.reshape(groups, group, rows, LANES).transpose(2, 0, 1, 3).reshape(rows, width)
    return out.astype(values.dtype)


def per_device(
    magnetic_potential_input,
    node_reordering,
    adjacent_dense_blocks,
    adjacent_cluster_pairs,
    distant_row_factors,
    distant_row_factor_index,
    distant_column_factors,
    distant_column_factor_index,
):
    row_count = lax.axis_size("row")
    col_count = lax.axis_size("col")
    row_index = lax.axis_index("row")
    col_index = lax.axis_index("col")
    local_states, width = magnetic_potential_input.shape
    states = local_states * row_count
    leaf = adjacent_dense_blocks.shape[1]
    rank = distant_row_factors.shape[2]
    cluster_extent = width // leaf
    row_span = cluster_extent * col_count // row_count
    window = 0
    for target in range(row_count):
        base_t = target * row_span - target * col_count // row_count * cluster_extent
        low_t = max(base_t - REACH, 0)
        high_t = min(base_t + row_span + REACH, cluster_extent)
        window = max(window, high_t - low_t)
    while (local_states * window * leaf) % (SUBLANES * 2 * LANES) and window < cluster_extent:
        window += 1
    block_entries = 4 * BL

    mine = reorder(magnetic_potential_input, node_reordering - col_index * width)

    dense = (SUBLANES * 2, local_states * width // (SUBLANES * 2))
    ordered = lax.all_gather(mine.reshape(dense), "row", axis=0, tiled=True)
    leaf_clusters = ordered.reshape(states, cluster_extent, leaf)

    every_block = lax.all_to_all(
        jnp.tile(mine.reshape(dense), (col_count, 1)), "col", 0, 0, tiled=True
    ).reshape(col_count, local_states, width)
    pieces = []
    for target in range(row_count):
        home_t = target * col_count // row_count
        start_t = min(max(target * row_span - home_t * cluster_extent - REACH, 0), cluster_extent - window)
        pieces.append(every_block[home_t, :, start_t * leaf:(start_t + window) * leaf])
    send = jnp.stack(pieces)
    if (local_states * window * leaf) % (SUBLANES * 2 * LANES) == 0:
        send = send.reshape(row_count * SUBLANES * 2, -1)
    near_window = lax.all_to_all(send, "row", 0, 0, tiled=True).reshape(states, window, leaf)

    home = row_index * col_count // row_count
    start = jnp.clip(row_index * row_span - home * cluster_extent - REACH, 0, cluster_extent - window)
    near_cols = adjacent_cluster_pairs[:, 1] - home * cluster_extent - start
    near_rows = adjacent_cluster_pairs[:, 0] - row_index * row_span
    near_src = jnp.take(near_window, near_cols, axis=1)
    near_out = jnp.einsum(
        "snk,nlk->nsl", near_src, adjacent_dense_blocks, preferred_element_type=jnp.float32
    )

    v_src = jnp.take(leaf_clusters, distant_column_factor_index[:, 0] - col_index * cluster_extent, axis=1)
    coeffs = jnp.einsum(
        "spk,pkr->psr", v_src, distant_column_factors, preferred_element_type=jnp.float32
    )
    fragments = coeffs.shape[0]
    column_indicator = (
        distant_column_factor_index[:, 1][None, :]
        == jnp.arange(block_entries, dtype=jnp.int32)[:, None]
    ).astype(jnp.float32)
    summed = jnp.dot(
        column_indicator,
        coeffs.reshape(fragments, states * rank),
        precision=lax.Precision.HIGHEST,
    ).astype(jnp.bfloat16).reshape(block_entries, states, rank)
    picked = jnp.take(summed, distant_row_factor_index[:, 1], axis=0)
    far_out = jnp.einsum(
        "psr,plr->psl", picked, distant_row_factors, preferred_element_type=jnp.float32
    )

    all_out = jnp.concatenate([near_out, far_out], axis=0)
    all_rows = jnp.concatenate([near_rows, distant_row_factor_index[:, 0] - row_index * row_span])
    scatter = (
        all_rows[None, :] == jnp.arange(row_span, dtype=jnp.int32)[:, None]
    ).astype(jnp.float32)
    partial_sum = jnp.dot(
        scatter,
        all_out.reshape(all_out.shape[0], states * leaf),
        precision=lax.Precision.HIGHEST,
    ).reshape(row_span, states, leaf)
    partial_sum = partial_sum.transpose(1, 0, 2).reshape(states, row_span * leaf)

    exchanged = lax.all_to_all(partial_sum, "col", 0, 0, tiled=True)
    return exchanged.reshape(col_count, states // col_count, row_span * leaf).sum(axis=0)


def solution(mesh):
    placed = (
        P("row", "col"),
        P("col"),
        P(("row", "col"), None, None),
        P(("row", "col"), None),
        P(("row", "col"), None, None),
        P(("row", "col"), None),
        P(("row", "col"), None, None),
        P(("row", "col"), None),
    )
    return jax.shard_map(
        per_device, mesh=mesh, in_specs=placed, out_specs=P("col", "row"), check_vma=False
    )
```

```python
import jax
import jax.numpy as jnp
from jax import lax
from jax.experimental import pallas as pl
from jax.experimental.pallas import tpu as pltpu
from jax.sharding import PartitionSpec as P

BL = 2
REACH = 3
LANES = 128
SUBLANES = 8
BATCH = 16


def _lane_gather_kernel(values_ref, order_ref, out_ref, doubled_ref):
    rows, width = values_ref.shape
    group = SUBLANES // rows
    tiles = width // LANES
    groups = tiles // group
    batch = min(BATCH, groups)
    for v in range(tiles):
        piece = values_ref[:, v * LANES:(v + 1) * LANES].astype(jnp.float32)
        doubled_ref[:, v * LANES:(v + 1) * LANES] = jnp.concatenate([piece] * group, axis=0)
    sub = lax.broadcasted_iota(jnp.int32, (SUBLANES, LANES), 0) // rows

    def group_body(k, carry):
        base = k * batch
        lows, highs = [], []
        for b in range(batch):
            first = (base + b) * group
            index = jnp.broadcast_to(order_ref[pl.ds(first, 1), :], (SUBLANES, LANES))
            for g in range(1, group):
                index = jnp.where(
                    sub == g, jnp.broadcast_to(order_ref[pl.ds(first + g, 1), :], (SUBLANES, LANES)), index
                )
            index = index % width
            lows.append(index % LANES)
            highs.append(index // LANES)

        def tile_body(v, accs):
            src = doubled_ref[:, pl.ds(pl.multiple_of(v * LANES, LANES), LANES)]
            return tuple(
                jnp.where(
                    highs[b] == v,
                    jnp.take_along_axis(src, lows[b], axis=1, mode="promise_in_bounds"),
                    accs[b],
                )
                for b in range(batch)
            )

        zeros = tuple(jnp.zeros((SUBLANES, LANES), jnp.float32) for _ in range(batch))
        accs = lax.fori_loop(0, tiles, tile_body, zeros)
        for b in range(batch):
            for g in range(group):
                column = pl.multiple_of(((base + b) * group + g) * LANES, LANES)
                out_ref[:, pl.ds(column, LANES)] = accs[b][g * rows:(g + 1) * rows, :]
        return carry

    lax.fori_loop(0, groups // batch, group_body, 0)


def reorder(values, order):
    rows, width = values.shape
    out = pl.pallas_call(
        _lane_gather_kernel,
        out_shape=jax.ShapeDtypeStruct((rows, width), jnp.float32),
        scratch_shapes=[pltpu.VMEM((SUBLANES, width), jnp.float32)],
    )(values, order.reshape(width // LANES, LANES))
    return out.astype(values.dtype)


def per_device(
    magnetic_potential_input,
    node_reordering,
    adjacent_dense_blocks,
    adjacent_cluster_pairs,
    distant_row_factors,
    distant_row_factor_index,
    distant_column_factors,
    distant_column_factor_index,
):
    row_count = lax.axis_size("row")
    col_count = lax.axis_size("col")
    row_index = lax.axis_index("row")
    col_index = lax.axis_index("col")
    local_states, width = magnetic_potential_input.shape
    states = local_states * row_count
    leaf = adjacent_dense_blocks.shape[1]
    rank = distant_row_factors.shape[2]
    cluster_extent = width // leaf
    row_span = cluster_extent * col_count // row_count
    window = 0
    for target in range(row_count):
        base_t = target * row_span - target * col_count // row_count * cluster_extent
        low_t = max(base_t - REACH, 0)
        high_t = min(base_t + row_span + REACH, cluster_extent)
        window = max(window, high_t - low_t)
    block_entries = 4 * BL

    mine = reorder(magnetic_potential_input, node_reordering)

    every_block = lax.all_to_all(jnp.tile(mine, (col_count, 1)), "col", 0, 0, tiled=True).reshape(
        col_count, local_states, width
    )
    pieces = []
    for target in range(row_count):
        home_t = target * col_count // row_count
        start_t = min(max(target * row_span - home_t * cluster_extent - REACH, 0), cluster_extent - window)
        pieces.append(every_block[home_t, :, start_t * leaf:(start_t + window) * leaf])
    send = jnp.concatenate(pieces, axis=0)
    mine_late, send = lax.optimization_barrier((mine, send))

    ordered = lax.all_gather(mine_late, "row", axis=0, tiled=True)
    leaf_clusters = ordered.reshape(states, cluster_extent, leaf)
    near_window = lax.all_to_all(send, "row", 0, 0, tiled=True).reshape(states, window, leaf)

    home = row_index * col_count // row_count
    start = jnp.clip(row_index * row_span - home * cluster_extent - REACH, 0, cluster_extent - window)
    near_cols = adjacent_cluster_pairs[:, 1] - home * cluster_extent - start
    near_rows = adjacent_cluster_pairs[:, 0] - row_index * row_span
    near_src = jnp.take(near_window, near_cols, axis=1)
    near_out = jnp.einsum(
        "snk,nlk->nsl", near_src, adjacent_dense_blocks, preferred_element_type=jnp.float32
    )

    v_src = jnp.take(leaf_clusters, distant_column_factor_index[:, 0] - col_index * cluster_extent, axis=1)
    coeffs = jnp.einsum(
        "spk,pkr->psr", v_src, distant_column_factors, preferred_element_type=jnp.float32
    )
    fragments = coeffs.shape[0]
    column_indicator = (
        distant_column_factor_index[:, 1][None, :]
        == jnp.arange(block_entries, dtype=jnp.int32)[:, None]
    ).astype(jnp.float32)
    summed = jnp.dot(
        column_indicator,
        coeffs.reshape(fragments, states * rank),
        precision=lax.Precision.HIGHEST,
    ).astype(jnp.bfloat16).reshape(block_entries, states, rank)
    picked = jnp.take(summed, distant_row_factor_index[:, 1], axis=0)
    far_out = jnp.einsum(
        "psr,plr->psl", picked, distant_row_factors, preferred_element_type=jnp.float32
    )

    all_out = jnp.concatenate([near_out, far_out], axis=0)
    all_rows = jnp.concatenate([near_rows, distant_row_factor_index[:, 0] - row_index * row_span])
    scatter = (
        all_rows[None, :] == jnp.arange(row_span, dtype=jnp.int32)[:, None]
    ).astype(jnp.float32)
    partial_sum = jnp.dot(
        scatter,
        all_out.reshape(all_out.shape[0], states * leaf),
        precision=lax.Precision.HIGHEST,
    ).reshape(row_span, states, leaf)
    partial_sum = partial_sum.transpose(1, 0, 2).reshape(states, row_span * leaf)

    exchanged = lax.all_to_all(partial_sum, "col", 0, 0, tiled=True)
    return exchanged.reshape(col_count, states // col_count, row_span * leaf).sum(axis=0)


def solution(mesh):
    placed = (
        P("row", "col"),
        P("col"),
        P(("row", "col"), None, None),
        P(("row", "col"), None),
        P(("row", "col"), None, None),
        P(("row", "col"), None),
        P(("row", "col"), None, None),
        P(("row", "col"), None),
    )
    return jax.shard_map(
        per_device, mesh=mesh, in_specs=placed, out_specs=P("col", "row"), check_vma=False
    )
```

```python
import jax
import jax.numpy as jnp
from jax import lax
from jax.experimental import pallas as pl
from jax.experimental.pallas import tpu as pltpu
from jax.sharding import PartitionSpec as P

BL = 2
REACH = 3
LANES = 128
SUBLANES = 8
BATCH = 16


def _lane_gather_kernel(values_ref, order_ref, out_ref, doubled_ref):
    rows, width = values_ref.shape
    group = SUBLANES // rows
    tiles = width // LANES
    groups = tiles // group
    batch = min(BATCH, groups)
    for v in range(tiles):
        piece = values_ref[:, v * LANES:(v + 1) * LANES].astype(jnp.float32)
        doubled_ref[:, v * LANES:(v + 1) * LANES] = jnp.concatenate([piece] * group, axis=0)
    sub = lax.broadcasted_iota(jnp.int32, (SUBLANES, LANES), 0) // rows

    def group_body(k, carry):
        base = k * batch
        lows, highs = [], []
        for b in range(batch):
            first = (base + b) * group
            index = jnp.broadcast_to(order_ref[pl.ds(first, 1), :], (SUBLANES, LANES))
            for g in range(1, group):
                index = jnp.where(
                    sub == g, jnp.broadcast_to(order_ref[pl.ds(first + g, 1), :], (SUBLANES, LANES)), index
                )
            index = index % width
            lows.append(index % LANES)
            highs.append(index // LANES)

        def tile_body(v, accs):
            src = doubled_ref[:, pl.ds(pl.multiple_of(v * LANES, LANES), LANES)]
            return tuple(
                jnp.where(
                    highs[b] == v,
                    jnp.take_along_axis(src, lows[b], axis=1, mode="promise_in_bounds"),
                    accs[b],
                )
                for b in range(batch)
            )

        zeros = tuple(jnp.zeros((SUBLANES, LANES), jnp.float32) for _ in range(batch))
        accs = lax.fori_loop(0, tiles, tile_body, zeros)
        for b in range(batch):
            for g in range(group):
                column = pl.multiple_of(((base + b) * group + g) * LANES, LANES)
                out_ref[:, pl.ds(column, LANES)] = accs[b][g * rows:(g + 1) * rows, :]
        return carry

    lax.fori_loop(0, groups // batch, group_body, 0)


def reorder(values, order):
    rows, width = values.shape
    out = pl.pallas_call(
        _lane_gather_kernel,
        out_shape=jax.ShapeDtypeStruct((rows, width), jnp.float32),
        scratch_shapes=[pltpu.VMEM((SUBLANES, width), jnp.float32)],
    )(values, order.reshape(width // LANES, LANES))
    return out.astype(values.dtype)


def per_device(
    magnetic_potential_input,
    node_reordering,
    adjacent_dense_blocks,
    adjacent_cluster_pairs,
    distant_row_factors,
    distant_row_factor_index,
    distant_column_factors,
    distant_column_factor_index,
):
    row_count = lax.axis_size("row")
    col_count = lax.axis_size("col")
    row_index = lax.axis_index("row")
    col_index = lax.axis_index("col")
    local_states, width = magnetic_potential_input.shape
    states = local_states * row_count
    leaf = adjacent_dense_blocks.shape[1]
    rank = distant_row_factors.shape[2]
    cluster_extent = width // leaf
    row_span = cluster_extent * col_count // row_count
    window = 0
    for target in range(row_count):
        base_t = target * row_span - target * col_count // row_count * cluster_extent
        low_t = max(base_t - REACH, 0)
        high_t = min(base_t + row_span + REACH, cluster_extent)
        window = max(window, high_t - low_t)
    block_entries = 4 * BL

    mine = reorder(magnetic_potential_input, node_reordering)

    every_block = lax.all_to_all(jnp.tile(mine, (col_count, 1)), "col", 0, 0, tiled=True).reshape(
        col_count, local_states, width
    )
    pieces = []
    for target in range(row_count):
        home_t = target * col_count // row_count
        start_t = min(max(target * row_span - home_t * cluster_extent - REACH, 0), cluster_extent - window)
        pieces.append(every_block[home_t, :, start_t * leaf:(start_t + window) * leaf])
    send = jnp.concatenate(pieces, axis=0)

    ordered = lax.all_gather(mine, "row", axis=0, tiled=True)
    leaf_clusters = ordered.reshape(states, cluster_extent, leaf)
    near_window = lax.all_to_all(send, "row", 0, 0, tiled=True).reshape(states, window, leaf)

    home = row_index * col_count // row_count
    start = jnp.clip(row_index * row_span - home * cluster_extent - REACH, 0, cluster_extent - window)
    near_cols = adjacent_cluster_pairs[:, 1] - home * cluster_extent - start
    near_rows = adjacent_cluster_pairs[:, 0] - row_index * row_span
    near_src = jnp.take(near_window, near_cols, axis=1)
    near_out = jnp.einsum(
        "snk,nlk->nsl", near_src, adjacent_dense_blocks, preferred_element_type=jnp.float32
    )

    v_src = jnp.take(leaf_clusters, distant_column_factor_index[:, 0] - col_index * cluster_extent, axis=1)
    coeffs = jnp.einsum(
        "spk,pkr->psr", v_src, distant_column_factors, preferred_element_type=jnp.float32
    )
    fragments = coeffs.shape[0]
    column_indicator = (
        distant_column_factor_index[:, 1][None, :]
        == jnp.arange(block_entries, dtype=jnp.int32)[:, None]
    ).astype(jnp.float32)
    summed = jnp.dot(
        column_indicator,
        coeffs.reshape(fragments, states * rank),
        precision=lax.Precision.HIGHEST,
    ).astype(jnp.bfloat16).reshape(block_entries, states, rank)
    picked = jnp.take(summed, distant_row_factor_index[:, 1], axis=0)
    far_out = jnp.einsum(
        "psr,plr->psl", picked, distant_row_factors, preferred_element_type=jnp.float32
    )

    all_out = jnp.concatenate([near_out, far_out], axis=0)
    all_rows = jnp.concatenate([near_rows, distant_row_factor_index[:, 0] - row_index * row_span])
    scatter = (
        all_rows[None, :] == jnp.arange(row_span, dtype=jnp.int32)[:, None]
    ).astype(jnp.float32)
    partial_sum = jnp.dot(
        scatter,
        all_out.reshape(all_out.shape[0], states * leaf),
        precision=lax.Precision.HIGHEST,
    ).reshape(row_span, states, leaf)
    partial_sum = partial_sum.transpose(1, 0, 2).reshape(states, row_span * leaf)

    exchanged = lax.all_to_all(partial_sum, "col", 0, 0, tiled=True)
    return exchanged.reshape(col_count, states // col_count, row_span * leaf).sum(axis=0)


def solution(mesh):
    placed = (
        P("row", "col"),
        P("col"),
        P(("row", "col"), None, None),
        P(("row", "col"), None),
        P(("row", "col"), None, None),
        P(("row", "col"), None),
        P(("row", "col"), None, None),
        P(("row", "col"), None),
    )
    return jax.shard_map(
        per_device, mesh=mesh, in_specs=placed, out_specs=P("col", "row"), check_vma=False
    )
```

```python
import jax
import jax.numpy as jnp
from jax import lax
from jax.experimental import pallas as pl
from jax.experimental.pallas import tpu as pltpu
from jax.sharding import PartitionSpec as P

BL = 2
REACH = 3
LANES = 128
SUBLANES = 8
BATCH = 16


def _lane_gather_kernel(values_ref, order_ref, out_ref, doubled_ref):
    rows, width = values_ref.shape
    group = SUBLANES // rows
    tiles = width // LANES
    groups = tiles // group
    batch = min(BATCH, groups)
    for v in range(tiles):
        piece = values_ref[:, v * LANES:(v + 1) * LANES].astype(jnp.float32)
        doubled_ref[:, v * LANES:(v + 1) * LANES] = jnp.concatenate([piece] * group, axis=0)
    sub = lax.broadcasted_iota(jnp.int32, (SUBLANES, LANES), 0) // rows

    def group_body(k, carry):
        base = k * batch
        lows, highs = [], []
        for b in range(batch):
            first = (base + b) * group
            index = jnp.broadcast_to(order_ref[pl.ds(first, 1), :], (SUBLANES, LANES))
            for g in range(1, group):
                index = jnp.where(
                    sub == g, jnp.broadcast_to(order_ref[pl.ds(first + g, 1), :], (SUBLANES, LANES)), index
                )
            index = index % width
            lows.append(index % LANES)
            highs.append(index // LANES)

        def tile_body(v, accs):
            src = doubled_ref[:, pl.ds(pl.multiple_of(v * LANES, LANES), LANES)]
            return tuple(
                jnp.where(
                    highs[b] == v,
                    jnp.take_along_axis(src, lows[b], axis=1, mode="promise_in_bounds"),
                    accs[b],
                )
                for b in range(batch)
            )

        zeros = tuple(jnp.zeros((SUBLANES, LANES), jnp.float32) for _ in range(batch))
        accs = lax.fori_loop(0, tiles, tile_body, zeros, unroll=True)
        for b in range(batch):
            for g in range(group):
                column = pl.multiple_of(((base + b) * group + g) * LANES, LANES)
                out_ref[:, pl.ds(column, LANES)] = accs[b][g * rows:(g + 1) * rows, :]
        return carry

    lax.fori_loop(0, groups // batch, group_body, 0)


def reorder(values, order):
    rows, width = values.shape
    out = pl.pallas_call(
        _lane_gather_kernel,
        out_shape=jax.ShapeDtypeStruct((rows, width), jnp.float32),
        scratch_shapes=[pltpu.VMEM((SUBLANES, width), jnp.float32)],
    )(values, order.reshape(width // LANES, LANES))
    return out.astype(values.dtype)


def per_device(
    magnetic_potential_input,
    node_reordering,
    adjacent_dense_blocks,
    adjacent_cluster_pairs,
    distant_row_factors,
    distant_row_factor_index,
    distant_column_factors,
    distant_column_factor_index,
):
    row_count = lax.axis_size("row")
    col_count = lax.axis_size("col")
    row_index = lax.axis_index("row")
    col_index = lax.axis_index("col")
    local_states, width = magnetic_potential_input.shape
    states = local_states * row_count
    leaf = adjacent_dense_blocks.shape[1]
    rank = distant_row_factors.shape[2]
    cluster_extent = width // leaf
    row_span = cluster_extent * col_count // row_count
    window = 0
    for target in range(row_count):
        base_t = target * row_span - target * col_count // row_count * cluster_extent
        low_t = max(base_t - REACH, 0)
        high_t = min(base_t + row_span + REACH, cluster_extent)
        window = max(window, high_t - low_t)
    block_entries = 4 * BL

    mine = reorder(magnetic_potential_input, node_reordering)

    every_block = lax.all_to_all(jnp.tile(mine, (col_count, 1)), "col", 0, 0, tiled=True).reshape(
        col_count, local_states, width
    )
    pieces = []
    for target in range(row_count):
        home_t = target * col_count // row_count
        start_t = min(max(target * row_span - home_t * cluster_extent - REACH, 0), cluster_extent - window)
        pieces.append(every_block[home_t, :, start_t * leaf:(start_t + window) * leaf])
    send = jnp.concatenate(pieces, axis=0)

    ordered = lax.all_gather(mine, "row", axis=0, tiled=True)
    leaf_clusters = ordered.reshape(states, cluster_extent, leaf)
    near_window = lax.all_to_all(send, "row", 0, 0, tiled=True).reshape(states, window, leaf)

    home = row_index * col_count // row_count
    start = jnp.clip(row_index * row_span - home * cluster_extent - REACH, 0, cluster_extent - window)
    near_cols = adjacent_cluster_pairs[:, 1] - home * cluster_extent - start
    near_rows = adjacent_cluster_pairs[:, 0] - row_index * row_span
    near_src = jnp.take(near_window, near_cols, axis=1)
    near_out = jnp.einsum(
        "snk,nlk->nsl", near_src, adjacent_dense_blocks, preferred_element_type=jnp.float32
    )

    v_src = jnp.take(leaf_clusters, distant_column_factor_index[:, 0] - col_index * cluster_extent, axis=1)
    coeffs = jnp.einsum(
        "spk,pkr->psr", v_src, distant_column_factors, preferred_element_type=jnp.float32
    )
    fragments = coeffs.shape[0]
    column_indicator = (
        distant_column_factor_index[:, 1][None, :]
        == jnp.arange(block_entries, dtype=jnp.int32)[:, None]
    ).astype(jnp.float32)
    summed = jnp.dot(
        column_indicator,
        coeffs.reshape(fragments, states * rank),
        precision=lax.Precision.HIGHEST,
    ).astype(jnp.bfloat16).reshape(block_entries, states, rank)
    picked = jnp.take(summed, distant_row_factor_index[:, 1], axis=0)
    far_out = jnp.einsum(
        "psr,plr->psl", picked, distant_row_factors, preferred_element_type=jnp.float32
    )

    all_out = jnp.concatenate([near_out, far_out], axis=0)
    all_rows = jnp.concatenate([near_rows, distant_row_factor_index[:, 0] - row_index * row_span])
    scatter = (
        all_rows[None, :] == jnp.arange(row_span, dtype=jnp.int32)[:, None]
    ).astype(jnp.float32)
    partial_sum = jnp.dot(
        scatter,
        all_out.reshape(all_out.shape[0], states * leaf),
        precision=lax.Precision.HIGHEST,
    ).reshape(row_span, states, leaf)
    partial_sum = partial_sum.transpose(1, 0, 2).reshape(states, row_span * leaf)

    exchanged = lax.all_to_all(partial_sum, "col", 0, 0, tiled=True)
    return exchanged.reshape(col_count, states // col_count, row_span * leaf).sum(axis=0)


def solution(mesh):
    placed = (
        P("row", "col"),
        P("col"),
        P(("row", "col"), None, None),
        P(("row", "col"), None),
        P(("row", "col"), None, None),
        P(("row", "col"), None),
        P(("row", "col"), None, None),
        P(("row", "col"), None),
    )
    return jax.shard_map(
        per_device, mesh=mesh, in_specs=placed, out_specs=P("col", "row"), check_vma=False
    )
```

```python
import jax
import jax.numpy as jnp
from jax import lax
from jax.experimental import pallas as pl
from jax.experimental.pallas import tpu as pltpu
from jax.sharding import PartitionSpec as P

BL = 2
REACH = 3
LANES = 128
SUBLANES = 8
BATCH = 16


def _lane_gather_kernel(values_ref, order_ref, out_ref, doubled_ref):
    rows, width = values_ref.shape
    group = SUBLANES // rows
    tiles = width // LANES
    groups = tiles // group
    batch = min(BATCH, groups)
    for v in range(tiles):
        piece = values_ref[:, v * LANES:(v + 1) * LANES].astype(jnp.float32)
        doubled_ref[:, v * LANES:(v + 1) * LANES] = jnp.concatenate([piece] * group, axis=0)
    sub = lax.broadcasted_iota(jnp.int32, (SUBLANES, LANES), 0) // rows

    def group_body(k, carry):
        base = k * batch
        lows, highs = [], []
        for b in range(batch):
            first = (base + b) * group
            index = jnp.broadcast_to(order_ref[pl.ds(first, 1), :], (SUBLANES, LANES))
            for g in range(1, group):
                index = jnp.where(
                    sub == g, jnp.broadcast_to(order_ref[pl.ds(first + g, 1), :], (SUBLANES, LANES)), index
                )
            index = index % width
            lows.append(index % LANES)
            highs.append(index // LANES)

        def tile_body(v, accs):
            src = doubled_ref[:, pl.ds(pl.multiple_of(v * LANES, LANES), LANES)]
            return tuple(
                jnp.where(
                    highs[b] == v,
                    jnp.take_along_axis(src, lows[b], axis=1, mode="promise_in_bounds"),
                    accs[b],
                )
                for b in range(batch)
            )

        zeros = tuple(jnp.zeros((SUBLANES, LANES), jnp.float32) for _ in range(batch))
        accs = lax.fori_loop(0, tiles, tile_body, zeros, unroll=True)
        for b in range(batch):
            for g in range(group):
                column = pl.multiple_of(((base + b) * group + g) * LANES, LANES)
                piece = accs[b][g * rows:(g + 1) * rows, :].astype(out_ref.dtype)
                for c in range(out_ref.shape[0]):
                    out_ref[c, :, pl.ds(column, LANES)] = piece
        return carry

    lax.fori_loop(0, groups // batch, group_body, 0)


def reorder(values, order, copies):
    rows, width = values.shape
    return pl.pallas_call(
        _lane_gather_kernel,
        out_shape=jax.ShapeDtypeStruct((copies, rows, width), values.dtype),
        scratch_shapes=[pltpu.VMEM((SUBLANES, width), jnp.float32)],
    )(values, order.reshape(width // LANES, LANES))


def per_device(
    magnetic_potential_input,
    node_reordering,
    adjacent_dense_blocks,
    adjacent_cluster_pairs,
    distant_row_factors,
    distant_row_factor_index,
    distant_column_factors,
    distant_column_factor_index,
):
    row_count = lax.axis_size("row")
    col_count = lax.axis_size("col")
    row_index = lax.axis_index("row")
    col_index = lax.axis_index("col")
    local_states, width = magnetic_potential_input.shape
    states = local_states * row_count
    leaf = adjacent_dense_blocks.shape[1]
    rank = distant_row_factors.shape[2]
    cluster_extent = width // leaf
    row_span = cluster_extent * col_count // row_count
    window = 0
    for target in range(row_count):
        base_t = target * row_span - target * col_count // row_count * cluster_extent
        low_t = max(base_t - REACH, 0)
        high_t = min(base_t + row_span + REACH, cluster_extent)
        window = max(window, high_t - low_t)
    block_entries = 4 * BL

    copies = reorder(magnetic_potential_input, node_reordering, col_count)
    mine = copies[0]

    every_block = lax.all_to_all(copies, "col", 0, 0, tiled=True)
    pieces = []
    for target in range(row_count):
        home_t = target * col_count // row_count
        start_t = min(max(target * row_span - home_t * cluster_extent - REACH, 0), cluster_extent - window)
        pieces.append(every_block[home_t, :, start_t * leaf:(start_t + window) * leaf])
    send = jnp.concatenate(pieces, axis=0)

    ordered = lax.all_gather(mine, "row", axis=0, tiled=True)
    leaf_clusters = ordered.reshape(states, cluster_extent, leaf)
    near_window = lax.all_to_all(send, "row", 0, 0, tiled=True).reshape(states, window, leaf)

    home = row_index * col_count // row_count
    start = jnp.clip(row_index * row_span - home * cluster_extent - REACH, 0, cluster_extent - window)
    near_cols = adjacent_cluster_pairs[:, 1] - home * cluster_extent - start
    near_rows = adjacent_cluster_pairs[:, 0] - row_index * row_span
    near_src = jnp.take(near_window, near_cols, axis=1)
    near_out = jnp.einsum(
        "snk,nlk->nsl", near_src, adjacent_dense_blocks, preferred_element_type=jnp.float32
    )

    v_src = jnp.take(leaf_clusters, distant_column_factor_index[:, 0] - col_index * cluster_extent, axis=1)
    coeffs = jnp.einsum(
        "spk,pkr->psr", v_src, distant_column_factors, preferred_element_type=jnp.float32
    )
    fragments = coeffs.shape[0]
    column_indicator = (
        distant_column_factor_index[:, 1][None, :]
        == jnp.arange(block_entries, dtype=jnp.int32)[:, None]
    ).astype(jnp.float32)
    summed = jnp.dot(
        column_indicator,
        coeffs.reshape(fragments, states * rank),
        precision=lax.Precision.HIGHEST,
    ).astype(jnp.bfloat16).reshape(block_entries, states, rank)
    picked = jnp.take(summed, distant_row_factor_index[:, 1], axis=0)
    far_out = jnp.einsum(
        "psr,plr->psl", picked, distant_row_factors, preferred_element_type=jnp.float32
    )

    def scatter_add(pieces, targets):
        onehot = (targets[None, :] == jnp.arange(row_span, dtype=jnp.int32)[:, None]).astype(jnp.float32)
        return jnp.dot(
            onehot, pieces.reshape(pieces.shape[0], states * leaf), precision=lax.Precision.HIGHEST
        ).reshape(row_span, states, leaf)

    far_sum = scatter_add(far_out, distant_row_factor_index[:, 0] - row_index * row_span)
    partial_sum = far_sum + scatter_add(near_out, near_rows)
    partial_sum = partial_sum.transpose(1, 0, 2).reshape(states, row_span * leaf)

    exchanged = lax.all_to_all(partial_sum, "col", 0, 0, tiled=True)
    return exchanged.reshape(col_count, states // col_count, row_span * leaf).sum(axis=0)


def solution(mesh):
    placed = (
        P("row", "col"),
        P("col"),
        P(("row", "col"), None, None),
        P(("row", "col"), None),
        P(("row", "col"), None, None),
        P(("row", "col"), None),
        P(("row", "col"), None, None),
        P(("row", "col"), None),
    )
    return jax.shard_map(
        per_device, mesh=mesh, in_specs=placed, out_specs=P("col", "row"), check_vma=False
    )
```

```python
import jax
import jax.numpy as jnp
from jax import lax
from jax.experimental import pallas as pl
from jax.experimental.pallas import tpu as pltpu
from jax.sharding import PartitionSpec as P

BL = 2
REACH = 3
LANES = 128
SUBLANES = 8
BATCH = 16


def _lane_gather_kernel(values_ref, order_ref, out_ref, doubled_ref):
    rows, width = values_ref.shape
    group = SUBLANES // rows
    tiles = width // LANES
    groups = tiles // group
    batch = min(BATCH, groups)
    for v in range(tiles):
        piece = values_ref[:, v * LANES:(v + 1) * LANES].astype(jnp.float32)
        doubled_ref[:, v * LANES:(v + 1) * LANES] = jnp.concatenate([piece] * group, axis=0)
    sub = lax.broadcasted_iota(jnp.int32, (SUBLANES, LANES), 0) // rows

    def group_body(k, carry):
        base = k * batch
        lows, highs = [], []
        for b in range(batch):
            first = (base + b) * group
            index = jnp.broadcast_to(order_ref[pl.ds(first, 1), :], (SUBLANES, LANES))
            for g in range(1, group):
                index = jnp.where(
                    sub == g, jnp.broadcast_to(order_ref[pl.ds(first + g, 1), :], (SUBLANES, LANES)), index
                )
            index = index % width
            lows.append(index % LANES)
            highs.append(index // LANES)

        def tile_body(v, accs):
            src = doubled_ref[:, pl.ds(pl.multiple_of(v * LANES, LANES), LANES)]
            return tuple(
                jnp.where(
                    highs[b] == v,
                    jnp.take_along_axis(src, lows[b], axis=1, mode="promise_in_bounds"),
                    accs[b],
                )
                for b in range(batch)
            )

        zeros = tuple(jnp.zeros((SUBLANES, LANES), jnp.float32) for _ in range(batch))
        accs = lax.fori_loop(0, tiles, tile_body, zeros, unroll=True)
        for b in range(batch):
            for g in range(group):
                column = pl.multiple_of(((base + b) * group + g) * LANES, LANES)
                out_ref[:, pl.ds(column, LANES)] = accs[b][g * rows:(g + 1) * rows, :].astype(out_ref.dtype)
        return carry

    lax.fori_loop(0, groups // batch, group_body, 0)


def reorder(values, order):
    rows, width = values.shape
    return pl.pallas_call(
        _lane_gather_kernel,
        out_shape=jax.ShapeDtypeStruct((rows, width), values.dtype),
        scratch_shapes=[pltpu.VMEM((SUBLANES, width), jnp.float32)],
    )(values, order.reshape(width // LANES, LANES))


def per_device(
    magnetic_potential_input,
    node_reordering,
    adjacent_dense_blocks,
    adjacent_cluster_pairs,
    distant_row_factors,
    distant_row_factor_index,
    distant_column_factors,
    distant_column_factor_index,
):
    row_count = lax.axis_size("row")
    col_count = lax.axis_size("col")
    row_index = lax.axis_index("row")
    col_index = lax.axis_index("col")
    local_states, width = magnetic_potential_input.shape
    states = local_states * row_count
    leaf = adjacent_dense_blocks.shape[1]
    rank = distant_row_factors.shape[2]
    cluster_extent = width // leaf
    row_span = cluster_extent * col_count // row_count
    window = 0
    for target in range(row_count):
        base_t = target * row_span - target * col_count // row_count * cluster_extent
        low_t = max(base_t - REACH, 0)
        high_t = min(base_t + row_span + REACH, cluster_extent)
        window = max(window, high_t - low_t)
    block_entries = 4 * BL

    mine = reorder(magnetic_potential_input, node_reordering)

    every_block = lax.all_to_all(jnp.tile(mine, (col_count, 1)), "col", 0, 0, tiled=True).reshape(
        col_count, local_states, width
    )
    pieces = []
    for target in range(row_count):
        home_t = target * col_count // row_count
        start_t = min(max(target * row_span - home_t * cluster_extent - REACH, 0), cluster_extent - window)
        pieces.append(every_block[home_t, :, start_t * leaf:(start_t + window) * leaf])
    send = jnp.concatenate(pieces, axis=0)

    ordered = lax.all_gather(mine, "row", axis=0, tiled=True)
    leaf_clusters = ordered.reshape(states, cluster_extent, leaf)
    near_window = lax.all_to_all(send, "row", 0, 0, tiled=True).reshape(states, window, leaf)

    home = row_index * col_count // row_count
    start = jnp.clip(row_index * row_span - home * cluster_extent - REACH, 0, cluster_extent - window)
    near_cols = adjacent_cluster_pairs[:, 1] - home * cluster_extent - start
    near_rows = adjacent_cluster_pairs[:, 0] - row_index * row_span
    near_src = jnp.take(near_window, near_cols, axis=1)
    near_out = jnp.einsum(
        "snk,nlk->nsl", near_src, adjacent_dense_blocks, preferred_element_type=jnp.float32
    )

    v_src = jnp.take(leaf_clusters, distant_column_factor_index[:, 0] - col_index * cluster_extent, axis=1)
    coeffs = jnp.einsum(
        "spk,pkr->psr", v_src, distant_column_factors, preferred_element_type=jnp.float32
    )
    fragments = coeffs.shape[0]
    column_indicator = (
        distant_column_factor_index[:, 1][None, :]
        == jnp.arange(block_entries, dtype=jnp.int32)[:, None]
    ).astype(jnp.float32)
    summed = jnp.dot(
        column_indicator,
        coeffs.reshape(fragments, states * rank),
        precision=lax.Precision.HIGHEST,
    ).astype(jnp.bfloat16).reshape(block_entries, states, rank)
    picked = jnp.take(summed, distant_row_factor_index[:, 1], axis=0)
    far_out = jnp.einsum(
        "psr,plr->psl", picked, distant_row_factors, preferred_element_type=jnp.float32
    )

    all_out = jnp.concatenate([near_out, far_out], axis=0)
    all_rows = jnp.concatenate([near_rows, distant_row_factor_index[:, 0] - row_index * row_span])
    scatter = (
        all_rows[None, :] == jnp.arange(row_span, dtype=jnp.int32)[:, None]
    ).astype(jnp.float32)
    partial_sum = jnp.dot(
        scatter,
        all_out.reshape(all_out.shape[0], states * leaf),
        precision=lax.Precision.HIGHEST,
    ).reshape(row_span, states, leaf)
    partial_sum = partial_sum.transpose(1, 0, 2).reshape(states, row_span * leaf)

    exchanged = lax.all_to_all(partial_sum, "col", 0, 0, tiled=True)
    return exchanged.reshape(col_count, states // col_count, row_span * leaf).sum(axis=0)


def solution(mesh):
    placed = (
        P("row", "col"),
        P("col"),
        P(("row", "col"), None, None),
        P(("row", "col"), None),
        P(("row", "col"), None, None),
        P(("row", "col"), None),
        P(("row", "col"), None, None),
        P(("row", "col"), None),
    )
    return jax.shard_map(
        per_device, mesh=mesh, in_specs=placed, out_specs=P("col", "row"), check_vma=False
    )
```

```python
import jax
import jax.numpy as jnp
from jax import lax
from jax.experimental import pallas as pl
from jax.experimental.pallas import tpu as pltpu
from jax.sharding import PartitionSpec as P

BL = 2
REACH = 3
LANES = 128
SUBLANES = 8
BATCH = 16


def _lane_gather_kernel(values_ref, order_ref, out_ref, doubled_ref):
    rows, width = values_ref.shape
    group = SUBLANES // rows
    tiles = width // LANES
    groups = tiles // group
    batch = min(BATCH, groups)
    for v in range(tiles):
        piece = values_ref[:, v * LANES:(v + 1) * LANES].astype(jnp.float32)
        doubled_ref[:, v * LANES:(v + 1) * LANES] = jnp.concatenate([piece] * group, axis=0)
    sub = lax.broadcasted_iota(jnp.int32, (SUBLANES, LANES), 0) // rows

    def group_body(k, carry):
        base = k * batch
        lows, highs = [], []
        for b in range(batch):
            first = (base + b) * group
            index = jnp.broadcast_to(order_ref[pl.ds(first, 1), :], (SUBLANES, LANES))
            for g in range(1, group):
                index = jnp.where(
                    sub == g, jnp.broadcast_to(order_ref[pl.ds(first + g, 1), :], (SUBLANES, LANES)), index
                )
            index = index % width
            lows.append(index % LANES)
            highs.append(index // LANES)

        def tile_body(v, accs):
            src = doubled_ref[:, pl.ds(pl.multiple_of(v * LANES, LANES), LANES)]
            return tuple(
                jnp.where(
                    highs[b] == v,
                    jnp.take_along_axis(src, lows[b], axis=1, mode="promise_in_bounds"),
                    accs[b],
                )
                for b in range(batch)
            )

        zeros = tuple(jnp.zeros((SUBLANES, LANES), jnp.float32) for _ in range(batch))
        accs = lax.fori_loop(0, tiles, tile_body, zeros, unroll=True)
        for b in range(batch):
            for g in range(group):
                column = pl.multiple_of(((base + b) * group + g) * LANES, LANES)
                out_ref[:, pl.ds(column, LANES)] = accs[b][g * rows:(g + 1) * rows, :].astype(out_ref.dtype)
        return carry

    lax.fori_loop(0, groups // batch, group_body, 0)


def reorder(values, order):
    rows, width = values.shape
    return pl.pallas_call(
        _lane_gather_kernel,
        out_shape=jax.ShapeDtypeStruct((rows, width), values.dtype),
        scratch_shapes=[pltpu.VMEM((SUBLANES, width), jnp.float32)],
    )(values, order.reshape(width // LANES, LANES))


def per_device(
    magnetic_potential_input,
    node_reordering,
    adjacent_dense_blocks,
    adjacent_cluster_pairs,
    distant_row_factors,
    distant_row_factor_index,
    distant_column_factors,
    distant_column_factor_index,
):
    row_count = lax.axis_size("row")
    col_count = lax.axis_size("col")
    row_index = lax.axis_index("row")
    col_index = lax.axis_index("col")
    local_states, width = magnetic_potential_input.shape
    states = local_states * row_count
    leaf = adjacent_dense_blocks.shape[1]
    rank = distant_row_factors.shape[2]
    cluster_extent = width // leaf
    row_span = cluster_extent * col_count // row_count
    window = 0
    for target in range(row_count):
        base_t = target * row_span - target * col_count // row_count * cluster_extent
        low_t = max(base_t - REACH, 0)
        high_t = min(base_t + row_span + REACH, cluster_extent)
        window = max(window, high_t - low_t)
    block_entries = 4 * BL

    mine = reorder(magnetic_potential_input, node_reordering)

    every_block = lax.all_to_all(jnp.tile(mine, (col_count, 1)), "col", 0, 0, tiled=True).reshape(
        col_count, local_states, width
    )
    pieces = []
    for target in range(row_count):
        home_t = target * col_count // row_count
        start_t = min(max(target * row_span - home_t * cluster_extent - REACH, 0), cluster_extent - window)
        pieces.append(every_block[home_t, :, start_t * leaf:(start_t + window) * leaf])
    send = jnp.concatenate(pieces, axis=0)
    mine_late, send = lax.optimization_barrier((mine, send))

    ordered = lax.all_gather(mine_late, "row", axis=0, tiled=True)
    leaf_clusters = ordered.reshape(states, cluster_extent, leaf)
    near_window = lax.all_to_all(send, "row", 0, 0, tiled=True).reshape(states, window, leaf)

    home = row_index * col_count // row_count
    start = jnp.clip(row_index * row_span - home * cluster_extent - REACH, 0, cluster_extent - window)
    near_cols = adjacent_cluster_pairs[:, 1] - home * cluster_extent - start
    near_rows = adjacent_cluster_pairs[:, 0] - row_index * row_span
    near_src = jnp.take(near_window, near_cols, axis=1)
    near_out = jnp.einsum(
        "snk,nlk->nsl", near_src, adjacent_dense_blocks, preferred_element_type=jnp.float32
    )

    v_src = jnp.take(leaf_clusters, distant_column_factor_index[:, 0] - col_index * cluster_extent, axis=1)
    coeffs = jnp.einsum(
        "spk,pkr->psr", v_src, distant_column_factors, preferred_element_type=jnp.float32
    )
    fragments = coeffs.shape[0]
    column_indicator = (
        distant_column_factor_index[:, 1][None, :]
        == jnp.arange(block_entries, dtype=jnp.int32)[:, None]
    ).astype(jnp.float32)
    summed = jnp.dot(
        column_indicator,
        coeffs.reshape(fragments, states * rank),
        precision=lax.Precision.HIGHEST,
    ).astype(jnp.bfloat16).reshape(block_entries, states, rank)
    picked = jnp.take(summed, distant_row_factor_index[:, 1], axis=0)
    far_out = jnp.einsum(
        "psr,plr->psl", picked, distant_row_factors, preferred_element_type=jnp.float32
    )

    all_out = jnp.concatenate([near_out, far_out], axis=0)
    all_rows = jnp.concatenate([near_rows, distant_row_factor_index[:, 0] - row_index * row_span])
    scatter = (
        all_rows[None, :] == jnp.arange(row_span, dtype=jnp.int32)[:, None]
    ).astype(jnp.float32)
    partial_sum = jnp.dot(
        scatter,
        all_out.reshape(all_out.shape[0], states * leaf),
        precision=lax.Precision.HIGHEST,
    ).reshape(row_span, states, leaf)
    partial_sum = partial_sum.transpose(1, 0, 2).reshape(states, row_span * leaf)

    exchanged = lax.all_to_all(partial_sum, "col", 0, 0, tiled=True)
    return exchanged.reshape(col_count, states // col_count, row_span * leaf).sum(axis=0)


def solution(mesh):
    placed = (
        P("row", "col"),
        P("col"),
        P(("row", "col"), None, None),
        P(("row", "col"), None),
        P(("row", "col"), None, None),
        P(("row", "col"), None),
        P(("row", "col"), None, None),
        P(("row", "col"), None),
    )
    return jax.shard_map(
        per_device, mesh=mesh, in_specs=placed, out_specs=P("col", "row"), check_vma=False
    )
```

```python
import jax
import jax.numpy as jnp
from jax import lax
from jax.experimental import pallas as pl
from jax.experimental.pallas import tpu as pltpu
from jax.sharding import PartitionSpec as P

BL = 2
REACH = 3
LANES = 128
SUBLANES = 8
BATCH = 16


def _lane_gather_kernel(values_ref, order_ref, out_ref, doubled_ref):
    rows, width = values_ref.shape
    group = SUBLANES // rows
    tiles = width // LANES
    groups = tiles // group
    batch = min(BATCH, groups)
    for v in range(tiles):
        piece = values_ref[:, v * LANES:(v + 1) * LANES].astype(jnp.float32)
        doubled_ref[:, v * LANES:(v + 1) * LANES] = jnp.concatenate([piece] * group, axis=0)
    sub = lax.broadcasted_iota(jnp.int32, (SUBLANES, LANES), 0) // rows

    def group_body(k, carry):
        base = k * batch
        lows, highs = [], []
        for b in range(batch):
            first = (base + b) * group
            index = jnp.broadcast_to(order_ref[pl.ds(first, 1), :], (SUBLANES, LANES))
            for g in range(1, group):
                index = jnp.where(
                    sub == g, jnp.broadcast_to(order_ref[pl.ds(first + g, 1), :], (SUBLANES, LANES)), index
                )
            index = index % width
            lows.append(index % LANES)
            highs.append(index // LANES)

        def tile_body(v, accs):
            src = doubled_ref[:, pl.ds(pl.multiple_of(v * LANES, LANES), LANES)]
            return tuple(
                jnp.where(
                    highs[b] == v,
                    jnp.take_along_axis(src, lows[b], axis=1, mode="promise_in_bounds"),
                    accs[b],
                )
                for b in range(batch)
            )

        zeros = tuple(jnp.zeros((SUBLANES, LANES), jnp.float32) for _ in range(batch))
        accs = lax.fori_loop(0, tiles, tile_body, zeros, unroll=True)
        for b in range(batch):
            for g in range(group):
                column = pl.multiple_of(((base + b) * group + g) * LANES, LANES)
                out_ref[:, pl.ds(column, LANES)] = accs[b][g * rows:(g + 1) * rows, :]
        return carry

    lax.fori_loop(0, groups // batch, group_body, 0)


def reorder(values, order):
    rows, width = values.shape
    out = pl.pallas_call(
        _lane_gather_kernel,
        out_shape=jax.ShapeDtypeStruct((rows, width), jnp.float32),
        scratch_shapes=[pltpu.VMEM((SUBLANES, width), jnp.float32)],
    )(values, order.reshape(width // LANES, LANES))
    return out.astype(values.dtype)


def per_device(
    magnetic_potential_input,
    node_reordering,
    adjacent_dense_blocks,
    adjacent_cluster_pairs,
    distant_row_factors,
    distant_row_factor_index,
    distant_column_factors,
    distant_column_factor_index,
):
    row_count = lax.axis_size("row")
    col_count = lax.axis_size("col")
    row_index = lax.axis_index("row")
    col_index = lax.axis_index("col")
    local_states, width = magnetic_potential_input.shape
    states = local_states * row_count
    leaf = adjacent_dense_blocks.shape[1]
    rank = distant_row_factors.shape[2]
    cluster_extent = width // leaf
    row_span = cluster_extent * col_count // row_count
    window = 0
    for target in range(row_count):
        base_t = target * row_span - target * col_count // row_count * cluster_extent
        low_t = max(base_t - REACH, 0)
        high_t = min(base_t + row_span + REACH, cluster_extent)
        window = max(window, high_t - low_t)
    block_entries = 4 * BL

    mine = reorder(magnetic_potential_input, node_reordering)

    every_block = lax.all_to_all(jnp.tile(mine, (col_count, 1)), "col", 0, 0, tiled=True).reshape(
        col_count, local_states, width
    )
    pieces = []
    for target in range(row_count):
        home_t = target * col_count // row_count
        start_t = min(max(target * row_span - home_t * cluster_extent - REACH, 0), cluster_extent - window)
        pieces.append(every_block[home_t, :, start_t * leaf:(start_t + window) * leaf])
    send = jnp.concatenate(pieces, axis=0)

    ordered = lax.all_gather(mine, "row", axis=0, tiled=True)
    leaf_clusters = ordered.reshape(states, cluster_extent, leaf)
    near_window = lax.all_to_all(send, "row", 0, 0, tiled=True).reshape(states, window, leaf)

    home = row_index * col_count // row_count
    start = jnp.clip(row_index * row_span - home * cluster_extent - REACH, 0, cluster_extent - window)
    near_cols = adjacent_cluster_pairs[:, 1] - home * cluster_extent - start
    near_rows = adjacent_cluster_pairs[:, 0] - row_index * row_span
    pick = (near_cols[:, None] == jnp.arange(window, dtype=jnp.int32)[None, :]).astype(near_window.dtype)
    near_src = jnp.einsum("nw,swk->snk", pick, near_window, preferred_element_type=jnp.float32).astype(
        near_window.dtype
    )
    near_out = jnp.einsum(
        "snk,nlk->nsl", near_src, adjacent_dense_blocks, preferred_element_type=jnp.float32
    )

    v_src = jnp.take(leaf_clusters, distant_column_factor_index[:, 0] - col_index * cluster_extent, axis=1)
    coeffs = jnp.einsum(
        "spk,pkr->psr", v_src, distant_column_factors, preferred_element_type=jnp.float32
    )
    fragments = coeffs.shape[0]
    column_indicator = (
        distant_column_factor_index[:, 1][None, :]
        == jnp.arange(block_entries, dtype=jnp.int32)[:, None]
    ).astype(jnp.float32)
    summed = jnp.dot(
        column_indicator,
        coeffs.reshape(fragments, states * rank),
        precision=lax.Precision.HIGHEST,
    ).astype(jnp.bfloat16).reshape(block_entries, states, rank)
    picked = jnp.take(summed, distant_row_factor_index[:, 1], axis=0)
    far_out = jnp.einsum(
        "psr,plr->psl", picked, distant_row_factors, preferred_element_type=jnp.float32
    )

    all_out = jnp.concatenate([near_out, far_out], axis=0)
    all_rows = jnp.concatenate([near_rows, distant_row_factor_index[:, 0] - row_index * row_span])
    scatter = (
        all_rows[None, :] == jnp.arange(row_span, dtype=jnp.int32)[:, None]
    ).astype(jnp.float32)
    partial_sum = jnp.dot(
        scatter,
        all_out.reshape(all_out.shape[0], states * leaf),
        precision=lax.Precision.HIGHEST,
    ).reshape(row_span, states, leaf)
    partial_sum = partial_sum.transpose(1, 0, 2).reshape(states, row_span * leaf)

    exchanged = lax.all_to_all(partial_sum, "col", 0, 0, tiled=True)
    return exchanged.reshape(col_count, states // col_count, row_span * leaf).sum(axis=0)


def solution(mesh):
    placed = (
        P("row", "col"),
        P("col"),
        P(("row", "col"), None, None),
        P(("row", "col"), None),
        P(("row", "col"), None, None),
        P(("row", "col"), None),
        P(("row", "col"), None, None),
        P(("row", "col"), None),
    )
    return jax.shard_map(
        per_device, mesh=mesh, in_specs=placed, out_specs=P("col", "row"), check_vma=False
    )
```

```python
import jax
import jax.numpy as jnp
from jax import lax
from jax.experimental import pallas as pl
from jax.experimental.pallas import tpu as pltpu
from jax.sharding import PartitionSpec as P

BL = 2
REACH = 3
LANES = 128
SUBLANES = 8
BATCH = 16


def _lane_gather_kernel(values_ref, order_ref, out_ref, doubled_ref):
    rows, width = values_ref.shape
    group = SUBLANES // rows
    tiles = width // LANES
    groups = tiles // group
    batch = min(BATCH, groups)
    for v in range(tiles):
        piece = values_ref[:, v * LANES:(v + 1) * LANES].astype(jnp.float32)
        doubled_ref[:, v * LANES:(v + 1) * LANES] = jnp.concatenate([piece] * group, axis=0)
    sub = lax.broadcasted_iota(jnp.int32, (SUBLANES, LANES), 0) // rows

    def group_body(k, carry):
        base = k * batch
        lows, highs = [], []
        for b in range(batch):
            first = (base + b) * group
            index = jnp.broadcast_to(order_ref[pl.ds(first, 1), :], (SUBLANES, LANES))
            for g in range(1, group):
                index = jnp.where(
                    sub == g, jnp.broadcast_to(order_ref[pl.ds(first + g, 1), :], (SUBLANES, LANES)), index
                )
            index = index % width
            lows.append(index % LANES)
            highs.append(index // LANES)

        def tile_body(v, accs):
            src = doubled_ref[:, pl.ds(pl.multiple_of(v * LANES, LANES), LANES)]
            return tuple(
                jnp.where(
                    highs[b] == v,
                    jnp.take_along_axis(src, lows[b], axis=1, mode="promise_in_bounds"),
                    accs[b],
                )
                for b in range(batch)
            )

        zeros = tuple(jnp.zeros((SUBLANES, LANES), jnp.float32) for _ in range(batch))
        accs = lax.fori_loop(0, tiles, tile_body, zeros, unroll=True)
        for b in range(batch):
            for g in range(group):
                column = pl.multiple_of(((base + b) * group + g) * LANES, LANES)
                out_ref[:, pl.ds(column, LANES)] = accs[b][g * rows:(g + 1) * rows, :]
        return carry

    lax.fori_loop(0, groups // batch, group_body, 0)


def reorder(values, order):
    rows, width = values.shape
    out = pl.pallas_call(
        _lane_gather_kernel,
        out_shape=jax.ShapeDtypeStruct((rows, width), jnp.float32),
        scratch_shapes=[pltpu.VMEM((SUBLANES, width), jnp.float32)],
    )(values, order.reshape(width // LANES, LANES))
    return out.astype(values.dtype)


def per_device(
    magnetic_potential_input,
    node_reordering,
    adjacent_dense_blocks,
    adjacent_cluster_pairs,
    distant_row_factors,
    distant_row_factor_index,
    distant_column_factors,
    distant_column_factor_index,
):
    row_count = lax.axis_size("row")
    col_count = lax.axis_size("col")
    row_index = lax.axis_index("row")
    col_index = lax.axis_index("col")
    local_states, width = magnetic_potential_input.shape
    states = local_states * row_count
    leaf = adjacent_dense_blocks.shape[1]
    rank = distant_row_factors.shape[2]
    cluster_extent = width // leaf
    row_span = cluster_extent * col_count // row_count
    window = 0
    for target in range(row_count):
        base_t = target * row_span - target * col_count // row_count * cluster_extent
        low_t = max(base_t - REACH, 0)
        high_t = min(base_t + row_span + REACH, cluster_extent)
        window = max(window, high_t - low_t)
    block_entries = 4 * BL

    mine = reorder(magnetic_potential_input, node_reordering)

    every_block = lax.all_to_all(jnp.tile(mine, (col_count, 1)), "col", 0, 0, tiled=True).reshape(
        col_count, local_states, width
    )
    pieces = []
    for target in range(row_count):
        home_t = target * col_count // row_count
        start_t = min(max(target * row_span - home_t * cluster_extent - REACH, 0), cluster_extent - window)
        pieces.append(every_block[home_t, :, start_t * leaf:(start_t + window) * leaf])
    send = jnp.concatenate(pieces, axis=0)

    ordered = lax.all_gather(mine, "row", axis=0, tiled=True)
    leaf_clusters = ordered.reshape(states, cluster_extent, leaf)
    near_window = lax.all_to_all(send, "row", 0, 0, tiled=True).reshape(states, window, leaf)

    home = row_index * col_count // row_count
    start = jnp.clip(row_index * row_span - home * cluster_extent - REACH, 0, cluster_extent - window)
    near_cols = adjacent_cluster_pairs[:, 1] - home * cluster_extent - start
    near_rows = adjacent_cluster_pairs[:, 0] - row_index * row_span
    pick = (near_cols[:, None] == jnp.arange(window, dtype=jnp.int32)[None, :]).astype(near_window.dtype)
    near_src = jnp.einsum("nw,swk->snk", pick, near_window, preferred_element_type=jnp.float32).astype(
        near_window.dtype
    )
    near_out = jnp.einsum(
        "snk,nlk->nsl", near_src, adjacent_dense_blocks, preferred_element_type=jnp.float32
    )

    v_pick = (
        (distant_column_factor_index[:, 0] - col_index * cluster_extent)[:, None]
        == jnp.arange(cluster_extent, dtype=jnp.int32)[None, :]
    ).astype(leaf_clusters.dtype)
    v_src = jnp.einsum("pc,sck->spk", v_pick, leaf_clusters, preferred_element_type=jnp.float32).astype(
        leaf_clusters.dtype
    )
    coeffs = jnp.einsum(
        "spk,pkr->psr", v_src, distant_column_factors, preferred_element_type=jnp.float32
    )
    fragments = coeffs.shape[0]
    column_indicator = (
        distant_column_factor_index[:, 1][None, :]
        == jnp.arange(block_entries, dtype=jnp.int32)[:, None]
    ).astype(jnp.float32)
    summed = jnp.dot(
        column_indicator,
        coeffs.reshape(fragments, states * rank),
        precision=lax.Precision.HIGHEST,
    ).astype(jnp.bfloat16).reshape(block_entries, states, rank)
    picked = jnp.take(summed, distant_row_factor_index[:, 1], axis=0)
    far_out = jnp.einsum(
        "psr,plr->psl", picked, distant_row_factors, preferred_element_type=jnp.float32
    )

    all_out = jnp.concatenate([near_out, far_out], axis=0)
    all_rows = jnp.concatenate([near_rows, distant_row_factor_index[:, 0] - row_index * row_span])
    scatter = (
        all_rows[None, :] == jnp.arange(row_span, dtype=jnp.int32)[:, None]
    ).astype(jnp.float32)
    partial_sum = jnp.dot(
        scatter,
        all_out.reshape(all_out.shape[0], states * leaf),
        precision=lax.Precision.HIGHEST,
    ).reshape(row_span, states, leaf)
    partial_sum = partial_sum.transpose(1, 0, 2).reshape(states, row_span * leaf)

    exchanged = lax.all_to_all(partial_sum, "col", 0, 0, tiled=True)
    return exchanged.reshape(col_count, states // col_count, row_span * leaf).sum(axis=0)


def solution(mesh):
    placed = (
        P("row", "col"),
        P("col"),
        P(("row", "col"), None, None),
        P(("row", "col"), None),
        P(("row", "col"), None, None),
        P(("row", "col"), None),
        P(("row", "col"), None, None),
        P(("row", "col"), None),
    )
    return jax.shard_map(
        per_device, mesh=mesh, in_specs=placed, out_specs=P("col", "row"), check_vma=False
    )
```

```python
import jax
import jax.numpy as jnp
from jax import lax
from jax.experimental import pallas as pl
from jax.experimental.pallas import tpu as pltpu
from jax.sharding import PartitionSpec as P

BL = 2
REACH = 3
LANES = 128
SUBLANES = 8
BATCH = 16


def _lane_gather_kernel(values_ref, order_ref, out_ref, doubled_ref):
    rows, width = values_ref.shape
    group = SUBLANES // rows
    tiles = width // LANES
    groups = tiles // group
    batch = min(BATCH, groups)
    for v in range(tiles):
        piece = values_ref[:, v * LANES:(v + 1) * LANES].astype(jnp.float32)
        doubled_ref[:, v * LANES:(v + 1) * LANES] = jnp.concatenate([piece] * group, axis=0)
    sub = lax.broadcasted_iota(jnp.int32, (SUBLANES, LANES), 0) // rows

    def group_body(k, carry):
        base = k * batch
        lows, highs = [], []
        for b in range(batch):
            first = (base + b) * group
            index = jnp.broadcast_to(order_ref[pl.ds(first, 1), :], (SUBLANES, LANES))
            for g in range(1, group):
                index = jnp.where(
                    sub == g, jnp.broadcast_to(order_ref[pl.ds(first + g, 1), :], (SUBLANES, LANES)), index
                )
            index = index % width
            lows.append(index % LANES)
            highs.append(index // LANES)

        def tile_body(v, accs):
            src = doubled_ref[:, pl.ds(pl.multiple_of(v * LANES, LANES), LANES)]
            return tuple(
                jnp.where(
                    highs[b] == v,
                    jnp.take_along_axis(src, lows[b], axis=1, mode="promise_in_bounds"),
                    accs[b],
                )
                for b in range(batch)
            )

        zeros = tuple(jnp.zeros((SUBLANES, LANES), jnp.float32) for _ in range(batch))
        accs = lax.fori_loop(0, tiles, tile_body, zeros, unroll=True)
        for b in range(batch):
            for g in range(group):
                column = pl.multiple_of(((base + b) * group + g) * LANES, LANES)
                out_ref[:, pl.ds(column, LANES)] = accs[b][g * rows:(g + 1) * rows, :].astype(out_ref.dtype)
        return carry

    lax.fori_loop(0, groups // batch, group_body, 0)


def reorder(values, order):
    rows, width = values.shape
    return pl.pallas_call(
        _lane_gather_kernel,
        out_shape=jax.ShapeDtypeStruct((rows, width), values.dtype),
        scratch_shapes=[pltpu.VMEM((SUBLANES, width), jnp.float32)],
    )(values, order.reshape(width // LANES, LANES))


def per_device(
    magnetic_potential_input,
    node_reordering,
    adjacent_dense_blocks,
    adjacent_cluster_pairs,
    distant_row_factors,
    distant_row_factor_index,
    distant_column_factors,
    distant_column_factor_index,
):
    row_count = lax.axis_size("row")
    col_count = lax.axis_size("col")
    row_index = lax.axis_index("row")
    col_index = lax.axis_index("col")
    local_states, width = magnetic_potential_input.shape
    states = local_states * row_count
    leaf = adjacent_dense_blocks.shape[1]
    rank = distant_row_factors.shape[2]
    cluster_extent = width // leaf
    row_span = cluster_extent * col_count // row_count
    window = 0
    for target in range(row_count):
        base_t = target * row_span - target * col_count // row_count * cluster_extent
        low_t = max(base_t - REACH, 0)
        high_t = min(base_t + row_span + REACH, cluster_extent)
        window = max(window, high_t - low_t)
    block_entries = 4 * BL

    mine = reorder(magnetic_potential_input, node_reordering)

    every_block = lax.all_to_all(jnp.tile(mine, (col_count, 1)), "col", 0, 0, tiled=True).reshape(
        col_count, local_states, width
    )
    pieces = []
    for target in range(row_count):
        home_t = target * col_count // row_count
        start_t = min(max(target * row_span - home_t * cluster_extent - REACH, 0), cluster_extent - window)
        pieces.append(every_block[home_t, :, start_t * leaf:(start_t + window) * leaf])
    send = jnp.concatenate(pieces, axis=0)

    ordered = lax.all_gather(mine, "row", axis=0, tiled=True)
    leaf_clusters = ordered.reshape(states, cluster_extent, leaf)
    near_window = lax.all_to_all(send, "row", 0, 0, tiled=True).reshape(states, window, leaf)

    home = row_index * col_count // row_count
    start = jnp.clip(row_index * row_span - home * cluster_extent - REACH, 0, cluster_extent - window)
    near_cols = adjacent_cluster_pairs[:, 1] - home * cluster_extent - start
    near_rows = adjacent_cluster_pairs[:, 0] - row_index * row_span
    pick = (near_cols[:, None] == jnp.arange(window, dtype=jnp.int32)[None, :]).astype(near_window.dtype)
    near_src = jnp.einsum("nw,swk->snk", pick, near_window, preferred_element_type=jnp.float32).astype(
        near_window.dtype
    )
    near_out = jnp.einsum(
        "snk,nlk->nsl", near_src, adjacent_dense_blocks, preferred_element_type=jnp.float32
    )

    v_pick = (
        (distant_column_factor_index[:, 0] - col_index * cluster_extent)[:, None]
        == jnp.arange(cluster_extent, dtype=jnp.int32)[None, :]
    ).astype(leaf_clusters.dtype)
    v_src = jnp.einsum("pc,sck->spk", v_pick, leaf_clusters, preferred_element_type=jnp.float32).astype(
        leaf_clusters.dtype
    )
    coeffs = jnp.einsum(
        "spk,pkr->psr", v_src, distant_column_factors, preferred_element_type=jnp.float32
    )
    fragments = coeffs.shape[0]
    column_indicator = (
        distant_column_factor_index[:, 1][None, :]
        == jnp.arange(block_entries, dtype=jnp.int32)[:, None]
    ).astype(jnp.float32)
    summed = jnp.dot(
        column_indicator,
        coeffs.reshape(fragments, states * rank),
        precision=lax.Precision.HIGHEST,
    ).astype(jnp.bfloat16).reshape(block_entries, states, rank)
    picked = jnp.take(summed, distant_row_factor_index[:, 1], axis=0)
    far_out = jnp.einsum(
        "psr,plr->psl", picked, distant_row_factors, preferred_element_type=jnp.float32
    )

    all_out = jnp.concatenate([near_out, far_out], axis=0)
    all_rows = jnp.concatenate([near_rows, distant_row_factor_index[:, 0] - row_index * row_span])
    scatter = (
        all_rows[None, :] == jnp.arange(row_span, dtype=jnp.int32)[:, None]
    ).astype(jnp.float32)
    partial_sum = jnp.dot(
        scatter,
        all_out.reshape(all_out.shape[0], states * leaf),
        precision=lax.Precision.HIGHEST,
    ).reshape(row_span, states, leaf)
    partial_sum = partial_sum.transpose(1, 0, 2).reshape(states, row_span * leaf)

    exchanged = lax.all_to_all(partial_sum, "col", 0, 0, tiled=True)
    return exchanged.reshape(col_count, states // col_count, row_span * leaf).sum(axis=0)


def solution(mesh):
    placed = (
        P("row", "col"),
        P("col"),
        P(("row", "col"), None, None),
        P(("row", "col"), None),
        P(("row", "col"), None, None),
        P(("row", "col"), None),
        P(("row", "col"), None, None),
        P(("row", "col"), None),
    )
    return jax.shard_map(
        per_device, mesh=mesh, in_specs=placed, out_specs=P("col", "row"), check_vma=False
    )
```

```python
import jax
import jax.numpy as jnp
from jax import lax
from jax.experimental import pallas as pl
from jax.experimental.pallas import tpu as pltpu
from jax.sharding import PartitionSpec as P

BL = 2
REACH = 3
LANES = 128
SUBLANES = 8
BATCH = 16


def _lane_gather_kernel(values_ref, order_ref, out_ref, copies_ref, doubled_ref):
    rows, width = values_ref.shape
    group = SUBLANES // rows
    tiles = width // LANES
    groups = tiles // group
    batch = min(BATCH, groups)
    for v in range(tiles):
        piece = values_ref[:, v * LANES:(v + 1) * LANES].astype(jnp.float32)
        doubled_ref[:, v * LANES:(v + 1) * LANES] = jnp.concatenate([piece] * group, axis=0)
    sub = lax.broadcasted_iota(jnp.int32, (SUBLANES, LANES), 0) // rows

    def group_body(k, carry):
        base = k * batch
        lows, highs = [], []
        for b in range(batch):
            first = (base + b) * group
            index = jnp.broadcast_to(order_ref[pl.ds(first, 1), :], (SUBLANES, LANES))
            for g in range(1, group):
                index = jnp.where(
                    sub == g, jnp.broadcast_to(order_ref[pl.ds(first + g, 1), :], (SUBLANES, LANES)), index
                )
            index = index % width
            lows.append(index % LANES)
            highs.append(index // LANES)

        def tile_body(v, accs):
            src = doubled_ref[:, pl.ds(pl.multiple_of(v * LANES, LANES), LANES)]
            return tuple(
                jnp.where(
                    highs[b] == v,
                    jnp.take_along_axis(src, lows[b], axis=1, mode="promise_in_bounds"),
                    accs[b],
                )
                for b in range(batch)
            )

        zeros = tuple(jnp.zeros((SUBLANES, LANES), jnp.float32) for _ in range(batch))
        accs = lax.fori_loop(0, tiles, tile_body, zeros, unroll=True)
        for b in range(batch):
            for g in range(group):
                column = pl.multiple_of(((base + b) * group + g) * LANES, LANES)
                piece = accs[b][g * rows:(g + 1) * rows, :].astype(out_ref.dtype)
                out_ref[:, pl.ds(column, LANES)] = piece
                for c in range(copies_ref.shape[0]):
                    copies_ref[c, :, pl.ds(column, LANES)] = piece
        return carry

    lax.fori_loop(0, groups // batch, group_body, 0)


def reorder(values, order, copies):
    rows, width = values.shape
    return pl.pallas_call(
        _lane_gather_kernel,
        out_shape=(
            jax.ShapeDtypeStruct((rows, width), values.dtype),
            jax.ShapeDtypeStruct((copies, rows, width), values.dtype),
        ),
        scratch_shapes=[pltpu.VMEM((SUBLANES, width), jnp.float32)],
    )(values, order.reshape(width // LANES, LANES))


def per_device(
    magnetic_potential_input,
    node_reordering,
    adjacent_dense_blocks,
    adjacent_cluster_pairs,
    distant_row_factors,
    distant_row_factor_index,
    distant_column_factors,
    distant_column_factor_index,
):
    row_count = lax.axis_size("row")
    col_count = lax.axis_size("col")
    row_index = lax.axis_index("row")
    col_index = lax.axis_index("col")
    local_states, width = magnetic_potential_input.shape
    states = local_states * row_count
    leaf = adjacent_dense_blocks.shape[1]
    rank = distant_row_factors.shape[2]
    cluster_extent = width // leaf
    row_span = cluster_extent * col_count // row_count
    window = 0
    for target in range(row_count):
        base_t = target * row_span - target * col_count // row_count * cluster_extent
        low_t = max(base_t - REACH, 0)
        high_t = min(base_t + row_span + REACH, cluster_extent)
        window = max(window, high_t - low_t)
    block_entries = 4 * BL

    mine, stacked = reorder(magnetic_potential_input, node_reordering, col_count)

    every_block = lax.all_to_all(stacked, "col", 0, 0, tiled=True)
    pieces = []
    for target in range(row_count):
        home_t = target * col_count // row_count
        start_t = min(max(target * row_span - home_t * cluster_extent - REACH, 0), cluster_extent - window)
        pieces.append(every_block[home_t, :, start_t * leaf:(start_t + window) * leaf])
    send = jnp.concatenate(pieces, axis=0)

    ordered = lax.all_gather(mine, "row", axis=0, tiled=True)
    leaf_clusters = ordered.reshape(states, cluster_extent, leaf)
    near_window = lax.all_to_all(send, "row", 0, 0, tiled=True).reshape(states, window, leaf)

    home = row_index * col_count // row_count
    start = jnp.clip(row_index * row_span - home * cluster_extent - REACH, 0, cluster_extent - window)
    near_cols = adjacent_cluster_pairs[:, 1] - home * cluster_extent - start
    near_rows = adjacent_cluster_pairs[:, 0] - row_index * row_span
    pick = (near_cols[:, None] == jnp.arange(window, dtype=jnp.int32)[None, :]).astype(near_window.dtype)
    near_src = jnp.einsum("nw,swk->snk", pick, near_window, preferred_element_type=jnp.float32).astype(
        near_window.dtype
    )
    near_out = jnp.einsum(
        "snk,nlk->nsl", near_src, adjacent_dense_blocks, preferred_element_type=jnp.float32
    )

    v_pick = (
        (distant_column_factor_index[:, 0] - col_index * cluster_extent)[:, None]
        == jnp.arange(cluster_extent, dtype=jnp.int32)[None, :]
    ).astype(leaf_clusters.dtype)
    v_src = jnp.einsum("pc,sck->spk", v_pick, leaf_clusters, preferred_element_type=jnp.float32).astype(
        leaf_clusters.dtype
    )
    coeffs = jnp.einsum(
        "spk,pkr->psr", v_src, distant_column_factors, preferred_element_type=jnp.float32
    )
    fragments = coeffs.shape[0]
    column_indicator = (
        distant_column_factor_index[:, 1][None, :]
        == jnp.arange(block_entries, dtype=jnp.int32)[:, None]
    ).astype(jnp.float32)
    summed = jnp.dot(
        column_indicator,
        coeffs.reshape(fragments, states * rank),
        precision=lax.Precision.HIGHEST,
    ).astype(jnp.bfloat16).reshape(block_entries, states, rank)
    picked = jnp.take(summed, distant_row_factor_index[:, 1], axis=0)
    far_out = jnp.einsum(
        "psr,plr->psl", picked, distant_row_factors, preferred_element_type=jnp.float32
    )

    all_out = jnp.concatenate([near_out, far_out], axis=0)
    all_rows = jnp.concatenate([near_rows, distant_row_factor_index[:, 0] - row_index * row_span])
    scatter = (
        all_rows[None, :] == jnp.arange(row_span, dtype=jnp.int32)[:, None]
    ).astype(jnp.float32)
    partial_sum = jnp.dot(
        scatter,
        all_out.reshape(all_out.shape[0], states * leaf),
        precision=lax.Precision.HIGHEST,
    ).reshape(row_span, states, leaf)
    partial_sum = partial_sum.transpose(1, 0, 2).reshape(states, row_span * leaf)

    exchanged = lax.all_to_all(partial_sum, "col", 0, 0, tiled=True)
    return exchanged.reshape(col_count, states // col_count, row_span * leaf).sum(axis=0)


def solution(mesh):
    placed = (
        P("row", "col"),
        P("col"),
        P(("row", "col"), None, None),
        P(("row", "col"), None),
        P(("row", "col"), None, None),
        P(("row", "col"), None),
        P(("row", "col"), None, None),
        P(("row", "col"), None),
    )
    return jax.shard_map(
        per_device, mesh=mesh, in_specs=placed, out_specs=P("col", "row"), check_vma=False
    )
```

```python
import jax
import jax.numpy as jnp
from jax import lax
from jax.experimental import pallas as pl
from jax.experimental.pallas import tpu as pltpu
from jax.sharding import PartitionSpec as P

BL = 2
REACH = 3
LANES = 128
SUBLANES = 8
BATCH = 16


def _lane_gather_kernel(values_ref, order_ref, out_ref, copies_ref, doubled_ref):
    rows, width = values_ref.shape
    group = SUBLANES // rows
    tiles = width // LANES
    groups = tiles // group
    batch = min(BATCH, groups)
    for v in range(tiles):
        piece = values_ref[:, v * LANES:(v + 1) * LANES].astype(jnp.float32)
        doubled_ref[:, v * LANES:(v + 1) * LANES] = jnp.concatenate([piece] * group, axis=0)
    sub = lax.broadcasted_iota(jnp.int32, (SUBLANES, LANES), 0) // rows

    def group_body(k, carry):
        base = k * batch
        lows, highs = [], []
        for b in range(batch):
            first = (base + b) * group
            index = jnp.broadcast_to(order_ref[pl.ds(first, 1), :], (SUBLANES, LANES))
            for g in range(1, group):
                index = jnp.where(
                    sub == g, jnp.broadcast_to(order_ref[pl.ds(first + g, 1), :], (SUBLANES, LANES)), index
                )
            index = index % width
            lows.append(index % LANES)
            highs.append(index // LANES)

        def tile_body(v, accs):
            src = doubled_ref[:, pl.ds(pl.multiple_of(v * LANES, LANES), LANES)]
            return tuple(
                jnp.where(
                    highs[b] == v,
                    jnp.take_along_axis(src, lows[b], axis=1, mode="promise_in_bounds"),
                    accs[b],
                )
                for b in range(batch)
            )

        zeros = tuple(jnp.zeros((SUBLANES, LANES), jnp.float32) for _ in range(batch))
        accs = lax.fori_loop(0, tiles, tile_body, zeros, unroll=True)
        for b in range(batch):
            for g in range(group):
                column = pl.multiple_of(((base + b) * group + g) * LANES, LANES)
                piece = accs[b][g * rows:(g + 1) * rows, :].astype(out_ref.dtype)
                out_ref[:, pl.ds(column, LANES)] = piece
                for c in range(copies_ref.shape[0]):
                    copies_ref[c, :, pl.ds(column, LANES)] = piece
        return carry

    lax.fori_loop(0, groups // batch, group_body, 0)


def reorder(values, order, copies):
    rows, width = values.shape
    return pl.pallas_call(
        _lane_gather_kernel,
        out_shape=(
            jax.ShapeDtypeStruct((rows, width), values.dtype),
            jax.ShapeDtypeStruct((copies, rows, width), values.dtype),
        ),
        scratch_shapes=[pltpu.VMEM((SUBLANES, width), jnp.float32)],
    )(values, order.reshape(width // LANES, LANES))


def per_device(
    magnetic_potential_input,
    node_reordering,
    adjacent_dense_blocks,
    adjacent_cluster_pairs,
    distant_row_factors,
    distant_row_factor_index,
    distant_column_factors,
    distant_column_factor_index,
):
    row_count = lax.axis_size("row")
    col_count = lax.axis_size("col")
    row_index = lax.axis_index("row")
    col_index = lax.axis_index("col")
    local_states, width = magnetic_potential_input.shape
    states = local_states * row_count
    leaf = adjacent_dense_blocks.shape[1]
    rank = distant_row_factors.shape[2]
    cluster_extent = width // leaf
    row_span = cluster_extent * col_count // row_count
    window = 0
    for target in range(row_count):
        base_t = target * row_span - target * col_count // row_count * cluster_extent
        low_t = max(base_t - REACH, 0)
        high_t = min(base_t + row_span + REACH, cluster_extent)
        window = max(window, high_t - low_t)
    block_entries = 4 * BL

    mine, stacked = reorder(magnetic_potential_input, node_reordering, col_count)

    every_block = lax.all_to_all(stacked, "col", 0, 0, tiled=True)
    pieces = []
    for target in range(row_count):
        home_t = target * col_count // row_count
        start_t = min(max(target * row_span - home_t * cluster_extent - REACH, 0), cluster_extent - window)
        pieces.append(every_block[home_t, :, start_t * leaf:(start_t + window) * leaf])
    send = jnp.concatenate(pieces, axis=0)

    ordered = lax.all_gather(mine, "row", axis=0, tiled=True)
    leaf_clusters = ordered.reshape(states, cluster_extent, leaf)
    near_window = lax.all_to_all(send, "row", 0, 0, tiled=True).reshape(states, window, leaf)

    home = row_index * col_count // row_count
    start = jnp.clip(row_index * row_span - home * cluster_extent - REACH, 0, cluster_extent - window)
    near_cols = adjacent_cluster_pairs[:, 1] - home * cluster_extent - start
    near_rows = adjacent_cluster_pairs[:, 0] - row_index * row_span
    pick = (near_cols[:, None] == jnp.arange(window, dtype=jnp.int32)[None, :]).astype(near_window.dtype)
    near_src = jnp.einsum("nw,swk->snk", pick, near_window, preferred_element_type=jnp.float32).astype(
        near_window.dtype
    )
    near_out = jnp.einsum(
        "snk,nlk->nsl", near_src, adjacent_dense_blocks, preferred_element_type=jnp.float32
    )

    v_pick = (
        (distant_column_factor_index[:, 0] - col_index * cluster_extent)[:, None]
        == jnp.arange(cluster_extent, dtype=jnp.int32)[None, :]
    ).astype(leaf_clusters.dtype)
    v_src = jnp.einsum("pc,sck->spk", v_pick, leaf_clusters, preferred_element_type=jnp.float32).astype(
        leaf_clusters.dtype
    )
    coeffs = jnp.einsum(
        "spk,pkr->psr", v_src, distant_column_factors, preferred_element_type=jnp.float32
    )
    fragments = coeffs.shape[0]
    column_indicator = (
        distant_column_factor_index[:, 1][None, :]
        == jnp.arange(block_entries, dtype=jnp.int32)[:, None]
    ).astype(jnp.float32)
    summed = jnp.dot(
        column_indicator,
        coeffs.reshape(fragments, states * rank),
        precision=lax.Precision.HIGHEST,
    ).astype(jnp.bfloat16).reshape(block_entries, states, rank)
    picked = jnp.take(summed, distant_row_factor_index[:, 1], axis=0)
    far_out = jnp.einsum(
        "psr,plr->psl", picked, distant_row_factors, preferred_element_type=jnp.float32
    )

    def scatter_add(pieces, targets):
        onehot = (targets[None, :] == jnp.arange(row_span, dtype=jnp.int32)[:, None]).astype(jnp.float32)
        return jnp.dot(
            onehot, pieces.reshape(pieces.shape[0], states * leaf), precision=lax.Precision.HIGHEST
        ).reshape(row_span, states, leaf)

    far_sum = scatter_add(far_out, distant_row_factor_index[:, 0] - row_index * row_span)
    partial_sum = far_sum + scatter_add(near_out, near_rows)
    partial_sum = partial_sum.transpose(1, 0, 2).reshape(states, row_span * leaf)

    exchanged = lax.all_to_all(partial_sum, "col", 0, 0, tiled=True)
    return exchanged.reshape(col_count, states // col_count, row_span * leaf).sum(axis=0)


def solution(mesh):
    placed = (
        P("row", "col"),
        P("col"),
        P(("row", "col"), None, None),
        P(("row", "col"), None),
        P(("row", "col"), None, None),
        P(("row", "col"), None),
        P(("row", "col"), None, None),
        P(("row", "col"), None),
    )
    return jax.shard_map(
        per_device, mesh=mesh, in_specs=placed, out_specs=P("col", "row"), check_vma=False
    )
```

```python
import jax
import jax.numpy as jnp
from jax import lax
from jax.experimental import pallas as pl
from jax.experimental.pallas import tpu as pltpu
from jax.sharding import PartitionSpec as P

BL = 2
REACH = 3
LANES = 128
SUBLANES = 8
BATCH = 16


def _lane_gather_kernel(values_ref, order_ref, out_ref, copies_ref, doubled_ref):
    rows, width = values_ref.shape
    group = SUBLANES // rows
    tiles = width // LANES
    groups = tiles // group
    batch = min(BATCH, groups)
    for v in range(tiles):
        piece = values_ref[:, v * LANES:(v + 1) * LANES].astype(jnp.float32)
        doubled_ref[:, v * LANES:(v + 1) * LANES] = jnp.concatenate([piece] * group, axis=0)
    sub = lax.broadcasted_iota(jnp.int32, (SUBLANES, LANES), 0) // rows

    def group_body(k, carry):
        base = k * batch
        lows, highs = [], []
        for b in range(batch):
            first = (base + b) * group
            index = jnp.broadcast_to(order_ref[pl.ds(first, 1), :], (SUBLANES, LANES))
            for g in range(1, group):
                index = jnp.where(
                    sub == g, jnp.broadcast_to(order_ref[pl.ds(first + g, 1), :], (SUBLANES, LANES)), index
                )
            index = index % width
            lows.append(index % LANES)
            highs.append(index // LANES)

        def tile_body(v, accs):
            src = doubled_ref[:, pl.ds(pl.multiple_of(v * LANES, LANES), LANES)]
            return tuple(
                jnp.where(
                    highs[b] == v,
                    jnp.take_along_axis(src, lows[b], axis=1, mode="promise_in_bounds"),
                    accs[b],
                )
                for b in range(batch)
            )

        zeros = tuple(jnp.zeros((SUBLANES, LANES), jnp.float32) for _ in range(batch))
        accs = lax.fori_loop(0, tiles, tile_body, zeros, unroll=True)
        for b in range(batch):
            for g in range(group):
                column = pl.multiple_of(((base + b) * group + g) * LANES, LANES)
                piece = accs[b][g * rows:(g + 1) * rows, :].astype(out_ref.dtype)
                out_ref[:, pl.ds(column, LANES)] = piece
                for c in range(copies_ref.shape[0]):
                    copies_ref[c, :, pl.ds(column, LANES)] = piece
        return carry

    lax.fori_loop(0, groups // batch, group_body, 0)


def reorder(values, order, copies):
    rows, width = values.shape
    return pl.pallas_call(
        _lane_gather_kernel,
        out_shape=(
            jax.ShapeDtypeStruct((rows, width), values.dtype),
            jax.ShapeDtypeStruct((copies, rows, width), values.dtype),
        ),
        scratch_shapes=[pltpu.VMEM((SUBLANES, width), jnp.float32)],
    )(values, order.reshape(width // LANES, LANES))


def per_device(
    magnetic_potential_input,
    node_reordering,
    adjacent_dense_blocks,
    adjacent_cluster_pairs,
    distant_row_factors,
    distant_row_factor_index,
    distant_column_factors,
    distant_column_factor_index,
):
    row_count = lax.axis_size("row")
    col_count = lax.axis_size("col")
    row_index = lax.axis_index("row")
    col_index = lax.axis_index("col")
    local_states, width = magnetic_potential_input.shape
    states = local_states * row_count
    leaf = adjacent_dense_blocks.shape[1]
    rank = distant_row_factors.shape[2]
    cluster_extent = width // leaf
    row_span = cluster_extent * col_count // row_count
    window = 0
    for target in range(row_count):
        base_t = target * row_span - target * col_count // row_count * cluster_extent
        low_t = max(base_t - REACH, 0)
        high_t = min(base_t + row_span + REACH, cluster_extent)
        window = max(window, high_t - low_t)
    block_entries = 4 * BL

    mine, stacked = reorder(magnetic_potential_input, node_reordering, col_count)

    every_block = lax.all_to_all(stacked, "col", 0, 0, tiled=True)
    pieces = []
    for target in range(row_count):
        home_t = target * col_count // row_count
        start_t = min(max(target * row_span - home_t * cluster_extent - REACH, 0), cluster_extent - window)
        pieces.append(every_block[home_t, :, start_t * leaf:(start_t + window) * leaf])
    send = jnp.concatenate(pieces, axis=0)

    ordered = lax.all_gather(mine, "row", axis=0, tiled=True)
    leaf_clusters = ordered.reshape(states, cluster_extent, leaf)
    near_window = lax.all_to_all(send, "row", 0, 0, tiled=True).reshape(states, window, leaf)

    home = row_index * col_count // row_count
    start = jnp.clip(row_index * row_span - home * cluster_extent - REACH, 0, cluster_extent - window)
    near_cols = adjacent_cluster_pairs[:, 1] - home * cluster_extent - start
    near_rows = adjacent_cluster_pairs[:, 0] - row_index * row_span
    pick = (near_cols[:, None] == jnp.arange(window, dtype=jnp.int32)[None, :]).astype(near_window.dtype)
    near_src = jnp.einsum("nw,swk->snk", pick, near_window, preferred_element_type=jnp.float32).astype(
        near_window.dtype
    )
    near_out = jnp.einsum(
        "snk,nlk->nsl", near_src, adjacent_dense_blocks, preferred_element_type=jnp.float32
    )

    v_pick = (
        (distant_column_factor_index[:, 0] - col_index * cluster_extent)[:, None]
        == jnp.arange(cluster_extent, dtype=jnp.int32)[None, :]
    ).astype(leaf_clusters.dtype)
    v_src = jnp.einsum("pc,sck->spk", v_pick, leaf_clusters, preferred_element_type=jnp.float32).astype(
        leaf_clusters.dtype
    )
    coeffs = jnp.einsum(
        "spk,pkr->psr", v_src, distant_column_factors, preferred_element_type=jnp.float32
    )
    fragments = coeffs.shape[0]
    column_indicator = (
        distant_column_factor_index[:, 1][None, :]
        == jnp.arange(block_entries, dtype=jnp.int32)[:, None]
    ).astype(jnp.float32)
    summed = jnp.dot(
        column_indicator,
        coeffs.reshape(fragments, states * rank),
        precision=lax.Precision.HIGHEST,
    ).astype(jnp.bfloat16).reshape(block_entries, states, rank)
    picked = jnp.take(summed, distant_row_factor_index[:, 1], axis=0)
    far_out = jnp.einsum(
        "psr,plr->psl", picked, distant_row_factors, preferred_element_type=jnp.float32
    )

    all_out = jnp.concatenate([near_out, far_out], axis=0)
    all_rows = jnp.concatenate([near_rows, distant_row_factor_index[:, 0] - row_index * row_span])
    scatter = (
        all_rows[None, :] == jnp.arange(row_span, dtype=jnp.int32)[:, None]
    ).astype(jnp.float32)
    partial_sum = jnp.dot(
        scatter,
        all_out.reshape(all_out.shape[0], states * leaf),
        precision=lax.Precision.HIGH,
    ).reshape(row_span, states, leaf)
    partial_sum = partial_sum.transpose(1, 0, 2).reshape(states, row_span * leaf)

    exchanged = lax.all_to_all(partial_sum, "col", 0, 0, tiled=True)
    return exchanged.reshape(col_count, states // col_count, row_span * leaf).sum(axis=0)


def solution(mesh):
    placed = (
        P("row", "col"),
        P("col"),
        P(("row", "col"), None, None),
        P(("row", "col"), None),
        P(("row", "col"), None, None),
        P(("row", "col"), None),
        P(("row", "col"), None, None),
        P(("row", "col"), None),
    )
    return jax.shard_map(
        per_device, mesh=mesh, in_specs=placed, out_specs=P("col", "row"), check_vma=False
    )
```

```python
import jax
import jax.numpy as jnp
from jax import lax
from jax.experimental import pallas as pl
from jax.experimental.pallas import tpu as pltpu
from jax.sharding import PartitionSpec as P

BL = 2
REACH = 3
LANES = 128
SUBLANES = 8
BATCH = 8


def _lane_gather_kernel(values_ref, order_ref, out_ref, copies_ref, doubled_ref):
    rows, width = values_ref.shape
    group = SUBLANES // rows
    tiles = width // LANES
    groups = tiles // group
    batch = min(BATCH, groups)
    for v in range(tiles):
        piece = values_ref[:, v * LANES:(v + 1) * LANES].astype(jnp.float32)
        doubled_ref[:, v * LANES:(v + 1) * LANES] = jnp.concatenate([piece] * group, axis=0)
    sub = lax.broadcasted_iota(jnp.int32, (SUBLANES, LANES), 0) // rows

    def group_body(k, carry):
        base = k * batch
        lows, highs = [], []
        for b in range(batch):
            first = (base + b) * group
            index = jnp.broadcast_to(order_ref[pl.ds(first, 1), :], (SUBLANES, LANES))
            for g in range(1, group):
                index = jnp.where(
                    sub == g, jnp.broadcast_to(order_ref[pl.ds(first + g, 1), :], (SUBLANES, LANES)), index
                )
            index = index % width
            lows.append(index % LANES)
            highs.append(index // LANES)

        def tile_body(v, accs):
            src = doubled_ref[:, pl.ds(pl.multiple_of(v * LANES, LANES), LANES)]
            return tuple(
                jnp.where(
                    highs[b] == v,
                    jnp.take_along_axis(src, lows[b], axis=1, mode="promise_in_bounds"),
                    accs[b],
                )
                for b in range(batch)
            )

        zeros = tuple(jnp.zeros((SUBLANES, LANES), jnp.float32) for _ in range(batch))
        accs = lax.fori_loop(0, tiles, tile_body, zeros, unroll=True)
        for b in range(batch):
            for g in range(group):
                column = pl.multiple_of(((base + b) * group + g) * LANES, LANES)
                piece = accs[b][g * rows:(g + 1) * rows, :].astype(out_ref.dtype)
                out_ref[:, pl.ds(column, LANES)] = piece
                for c in range(copies_ref.shape[0]):
                    copies_ref[c, :, pl.ds(column, LANES)] = piece
        return carry

    lax.fori_loop(0, groups // batch, group_body, 0)


def reorder(values, order, copies):
    rows, width = values.shape
    return pl.pallas_call(
        _lane_gather_kernel,
        out_shape=(
            jax.ShapeDtypeStruct((rows, width), values.dtype),
            jax.ShapeDtypeStruct((copies, rows, width), values.dtype),
        ),
        scratch_shapes=[pltpu.VMEM((SUBLANES, width), jnp.float32)],
    )(values, order.reshape(width // LANES, LANES))


def per_device(
    magnetic_potential_input,
    node_reordering,
    adjacent_dense_blocks,
    adjacent_cluster_pairs,
    distant_row_factors,
    distant_row_factor_index,
    distant_column_factors,
    distant_column_factor_index,
):
    row_count = lax.axis_size("row")
    col_count = lax.axis_size("col")
    row_index = lax.axis_index("row")
    col_index = lax.axis_index("col")
    local_states, width = magnetic_potential_input.shape
    states = local_states * row_count
    leaf = adjacent_dense_blocks.shape[1]
    rank = distant_row_factors.shape[2]
    cluster_extent = width // leaf
    row_span = cluster_extent * col_count // row_count
    window = 0
    for target in range(row_count):
        base_t = target * row_span - target * col_count // row_count * cluster_extent
        low_t = max(base_t - REACH, 0)
        high_t = min(base_t + row_span + REACH, cluster_extent)
        window = max(window, high_t - low_t)
    block_entries = 4 * BL

    mine, stacked = reorder(magnetic_potential_input, node_reordering, col_count)

    every_block = lax.all_to_all(stacked, "col", 0, 0, tiled=True)
    pieces = []
    for target in range(row_count):
        home_t = target * col_count // row_count
        start_t = min(max(target * row_span - home_t * cluster_extent - REACH, 0), cluster_extent - window)
        pieces.append(every_block[home_t, :, start_t * leaf:(start_t + window) * leaf])
    send = jnp.concatenate(pieces, axis=0)

    ordered = lax.all_gather(mine, "row", axis=0, tiled=True)
    leaf_clusters = ordered.reshape(states, cluster_extent, leaf)
    near_window = lax.all_to_all(send, "row", 0, 0, tiled=True).reshape(states, window, leaf)

    home = row_index * col_count // row_count
    start = jnp.clip(row_index * row_span - home * cluster_extent - REACH, 0, cluster_extent - window)
    near_cols = adjacent_cluster_pairs[:, 1] - home * cluster_extent - start
    near_rows = adjacent_cluster_pairs[:, 0] - row_index * row_span
    pick = (near_cols[:, None] == jnp.arange(window, dtype=jnp.int32)[None, :]).astype(near_window.dtype)
    near_src = jnp.einsum("nw,swk->snk", pick, near_window, preferred_element_type=jnp.float32).astype(
        near_window.dtype
    )
    near_out = jnp.einsum(
        "snk,nlk->nsl", near_src, adjacent_dense_blocks, preferred_element_type=jnp.float32
    )

    v_pick = (
        (distant_column_factor_index[:, 0] - col_index * cluster_extent)[:, None]
        == jnp.arange(cluster_extent, dtype=jnp.int32)[None, :]
    ).astype(leaf_clusters.dtype)
    v_src = jnp.einsum("pc,sck->spk", v_pick, leaf_clusters, preferred_element_type=jnp.float32).astype(
        leaf_clusters.dtype
    )
    coeffs = jnp.einsum(
        "spk,pkr->psr", v_src, distant_column_factors, preferred_element_type=jnp.float32
    )
    fragments = coeffs.shape[0]
    column_indicator = (
        distant_column_factor_index[:, 1][None, :]
        == jnp.arange(block_entries, dtype=jnp.int32)[:, None]
    ).astype(jnp.float32)
    summed = jnp.dot(
        column_indicator,
        coeffs.reshape(fragments, states * rank),
        precision=lax.Precision.HIGHEST,
    ).astype(jnp.bfloat16).reshape(block_entries, states, rank)
    picked = jnp.take(summed, distant_row_factor_index[:, 1], axis=0)
    far_out = jnp.einsum(
        "psr,plr->psl", picked, distant_row_factors, preferred_element_type=jnp.float32
    )

    all_out = jnp.concatenate([near_out, far_out], axis=0)
    all_rows = jnp.concatenate([near_rows, distant_row_factor_index[:, 0] - row_index * row_span])
    scatter = (
        all_rows[None, :] == jnp.arange(row_span, dtype=jnp.int32)[:, None]
    ).astype(jnp.float32)
    partial_sum = jnp.dot(
        scatter,
        all_out.reshape(all_out.shape[0], states * leaf),
        precision=lax.Precision.HIGH,
    ).reshape(row_span, states, leaf)
    partial_sum = partial_sum.transpose(1, 0, 2).reshape(states, row_span * leaf)

    exchanged = lax.all_to_all(partial_sum, "col", 0, 0, tiled=True)
    return exchanged.reshape(col_count, states // col_count, row_span * leaf).sum(axis=0)


def solution(mesh):
    placed = (
        P("row", "col"),
        P("col"),
        P(("row", "col"), None, None),
        P(("row", "col"), None),
        P(("row", "col"), None, None),
        P(("row", "col"), None),
        P(("row", "col"), None, None),
        P(("row", "col"), None),
    )
    return jax.shard_map(
        per_device, mesh=mesh, in_specs=placed, out_specs=P("col", "row"), check_vma=False
    )
```

```python
import jax
import jax.numpy as jnp
from jax import lax
from jax.experimental import pallas as pl
from jax.experimental.pallas import tpu as pltpu
from jax.sharding import PartitionSpec as P

BL = 2
REACH = 3
LANES = 128
SUBLANES = 8
BATCH = 16


def _lane_gather_kernel(values_ref, order_ref, out_ref, copies_ref, doubled_ref):
    rows, width = values_ref.shape
    group = SUBLANES // rows
    tiles = width // LANES
    groups = tiles // group
    batch = min(BATCH, groups)
    for v in range(tiles):
        piece = values_ref[:, v * LANES:(v + 1) * LANES].astype(jnp.float32)
        doubled_ref[:, v * LANES:(v + 1) * LANES] = jnp.concatenate([piece] * group, axis=0)
    sub = lax.broadcasted_iota(jnp.int32, (SUBLANES, LANES), 0) // rows

    def group_body(k, carry):
        base = k * batch
        lows, highs = [], []
        for b in range(batch):
            first = (base + b) * group
            index = jnp.broadcast_to(order_ref[pl.ds(first, 1), :], (SUBLANES, LANES))
            for g in range(1, group):
                index = jnp.where(
                    sub == g, jnp.broadcast_to(order_ref[pl.ds(first + g, 1), :], (SUBLANES, LANES)), index
                )
            index = index % width
            lows.append(index % LANES)
            highs.append(index // LANES)

        def tile_body(v, accs):
            src = doubled_ref[:, pl.ds(pl.multiple_of(v * LANES, LANES), LANES)]
            return tuple(
                jnp.where(
                    highs[b] == v,
                    jnp.take_along_axis(src, lows[b], axis=1, mode="promise_in_bounds"),
                    accs[b],
                )
                for b in range(batch)
            )

        zeros = tuple(jnp.zeros((SUBLANES, LANES), jnp.float32) for _ in range(batch))
        accs = lax.fori_loop(0, tiles, tile_body, zeros, unroll=True)
        for b in range(batch):
            for g in range(group):
                column = pl.multiple_of(((base + b) * group + g) * LANES, LANES)
                piece = accs[b][g * rows:(g + 1) * rows, :].astype(out_ref.dtype)
                out_ref[:, pl.ds(column, LANES)] = piece
                for c in range(copies_ref.shape[0]):
                    copies_ref[c, :, pl.ds(column, LANES)] = piece
        return carry

    lax.fori_loop(0, groups // batch, group_body, 0)


def reorder(values, order, copies):
    rows, width = values.shape
    return pl.pallas_call(
        _lane_gather_kernel,
        out_shape=(
            jax.ShapeDtypeStruct((rows, width), values.dtype),
            jax.ShapeDtypeStruct((copies, rows, width), values.dtype),
        ),
        scratch_shapes=[pltpu.VMEM((SUBLANES, width), jnp.float32)],
    )(values, order.reshape(width // LANES, LANES))


def per_device(
    magnetic_potential_input,
    node_reordering,
    adjacent_dense_blocks,
    adjacent_cluster_pairs,
    distant_row_factors,
    distant_row_factor_index,
    distant_column_factors,
    distant_column_factor_index,
):
    row_count = lax.axis_size("row")
    col_count = lax.axis_size("col")
    row_index = lax.axis_index("row")
    col_index = lax.axis_index("col")
    local_states, width = magnetic_potential_input.shape
    states = local_states * row_count
    leaf = adjacent_dense_blocks.shape[1]
    rank = distant_row_factors.shape[2]
    cluster_extent = width // leaf
    row_span = cluster_extent * col_count // row_count
    window = 0
    for target in range(row_count):
        base_t = target * row_span - target * col_count // row_count * cluster_extent
        low_t = max(base_t - REACH, 0)
        high_t = min(base_t + row_span + REACH, cluster_extent)
        window = max(window, high_t - low_t)
    block_entries = 4 * BL

    mine, stacked = reorder(magnetic_potential_input, node_reordering, col_count)

    every_block = lax.all_to_all(stacked, "col", 0, 0, tiled=True)
    pieces = []
    for target in range(row_count):
        home_t = target * col_count // row_count
        start_t = min(max(target * row_span - home_t * cluster_extent - REACH, 0), cluster_extent - window)
        pieces.append(every_block[home_t, :, start_t * leaf:(start_t + window) * leaf])
    send = jnp.concatenate(pieces, axis=0)

    ordered = lax.all_gather(mine, "row", axis=0, tiled=True)
    leaf_clusters = ordered.reshape(states, cluster_extent, leaf)
    near_window = lax.all_to_all(send, "row", 0, 0, tiled=True).reshape(states, window, leaf)

    home = row_index * col_count // row_count
    start = jnp.clip(row_index * row_span - home * cluster_extent - REACH, 0, cluster_extent - window)
    near_cols = adjacent_cluster_pairs[:, 1] - home * cluster_extent - start
    pick = (near_cols[:, None] == jnp.arange(window, dtype=jnp.int32)[None, :]).astype(near_window.dtype)
    near_src = jnp.einsum("nw,swk->snk", pick, near_window, preferred_element_type=jnp.float32).astype(
        near_window.dtype
    )
    near_out = jnp.einsum(
        "snk,nlk->nsl", near_src, adjacent_dense_blocks, preferred_element_type=jnp.float32
    )

    v_pick = (
        distant_column_factor_index[:, 0][:, None]
        == (col_index * cluster_extent + jnp.arange(cluster_extent, dtype=jnp.int32))[None, :]
    ).astype(leaf_clusters.dtype)
    v_src = jnp.einsum("pc,sck->spk", v_pick, leaf_clusters, preferred_element_type=jnp.float32).astype(
        leaf_clusters.dtype
    )
    coeffs = jnp.einsum(
        "spk,pkr->psr", v_src, distant_column_factors, preferred_element_type=jnp.float32
    )
    fragments = coeffs.shape[0]
    column_indicator = (
        distant_column_factor_index[:, 1][None, :]
        == jnp.arange(block_entries, dtype=jnp.int32)[:, None]
    ).astype(jnp.float32)
    summed = jnp.dot(
        column_indicator,
        coeffs.reshape(fragments, states * rank),
        precision=lax.Precision.HIGHEST,
    ).astype(jnp.bfloat16).reshape(block_entries, states, rank)
    picked = jnp.take(summed, distant_row_factor_index[:, 1], axis=0)
    far_out = jnp.einsum(
        "psr,plr->psl", picked, distant_row_factors, preferred_element_type=jnp.float32
    )

    all_out = jnp.concatenate([near_out, far_out], axis=0)
    all_rows = jnp.concatenate([adjacent_cluster_pairs[:, 0], distant_row_factor_index[:, 0]])
    scatter = (
        all_rows[None, :] == (row_index * row_span + jnp.arange(row_span, dtype=jnp.int32))[:, None]
    ).astype(jnp.float32)
    partial_sum = jnp.dot(
        scatter,
        all_out.reshape(all_out.shape[0], states * leaf),
        precision=lax.Precision.HIGH,
    ).reshape(row_span, states, leaf)
    partial_sum = partial_sum.transpose(1, 0, 2).reshape(states, row_span * leaf)

    exchanged = lax.all_to_all(partial_sum, "col", 0, 0, tiled=True)
    return exchanged.reshape(col_count, states // col_count, row_span * leaf).sum(axis=0)


def solution(mesh):
    placed = (
        P("row", "col"),
        P("col"),
        P(("row", "col"), None, None),
        P(("row", "col"), None),
        P(("row", "col"), None, None),
        P(("row", "col"), None),
        P(("row", "col"), None, None),
        P(("row", "col"), None),
    )
    return jax.shard_map(
        per_device, mesh=mesh, in_specs=placed, out_specs=P("col", "row"), check_vma=False
    )
```

```python
import jax
import jax.numpy as jnp
from jax import lax
from jax.experimental import pallas as pl
from jax.experimental.pallas import tpu as pltpu
from jax.sharding import PartitionSpec as P

BL = 2
REACH = 3
LANES = 128
SUBLANES = 8
BATCH = 16


def _lane_gather_kernel(values_ref, order_ref, out_ref, copies_ref):
    rows, width = values_ref.shape
    group = SUBLANES // rows
    tiles = width // LANES
    groups = tiles // group
    batch = min(BATCH, groups)
    sub = lax.broadcasted_iota(jnp.int32, (SUBLANES, LANES), 0) // rows

    def group_body(k, carry):
        base = k * batch
        lows, highs = [], []
        for b in range(batch):
            first = (base + b) * group
            index = jnp.broadcast_to(order_ref[pl.ds(first, 1), :], (SUBLANES, LANES))
            for g in range(1, group):
                index = jnp.where(
                    sub == g, jnp.broadcast_to(order_ref[pl.ds(first + g, 1), :], (SUBLANES, LANES)), index
                )
            index = index % width
            lows.append(index % LANES)
            highs.append(index // LANES)

        def tile_body(v, accs):
            tile = values_ref[:, pl.ds(pl.multiple_of(v * LANES, LANES), LANES)].astype(jnp.float32)
            src = jnp.concatenate([tile] * group, axis=0)
            return tuple(
                jnp.where(
                    highs[b] == v,
                    jnp.take_along_axis(src, lows[b], axis=1, mode="promise_in_bounds"),
                    accs[b],
                )
                for b in range(batch)
            )

        zeros = tuple(jnp.zeros((SUBLANES, LANES), jnp.float32) for _ in range(batch))
        accs = lax.fori_loop(0, tiles, tile_body, zeros, unroll=True)
        for b in range(batch):
            for g in range(group):
                column = pl.multiple_of(((base + b) * group + g) * LANES, LANES)
                piece = accs[b][g * rows:(g + 1) * rows, :].astype(out_ref.dtype)
                out_ref[:, pl.ds(column, LANES)] = piece
                for c in range(copies_ref.shape[0]):
                    copies_ref[c, :, pl.ds(column, LANES)] = piece
        return carry

    lax.fori_loop(0, groups // batch, group_body, 0)


def reorder(values, order, copies):
    rows, width = values.shape
    return pl.pallas_call(
        _lane_gather_kernel,
        out_shape=(
            jax.ShapeDtypeStruct((rows, width), values.dtype),
            jax.ShapeDtypeStruct((copies, rows, width), values.dtype),
        ),
    )(values, order.reshape(width // LANES, LANES))


def per_device(
    magnetic_potential_input,
    node_reordering,
    adjacent_dense_blocks,
    adjacent_cluster_pairs,
    distant_row_factors,
    distant_row_factor_index,
    distant_column_factors,
    distant_column_factor_index,
):
    row_count = lax.axis_size("row")
    col_count = lax.axis_size("col")
    row_index = lax.axis_index("row")
    col_index = lax.axis_index("col")
    local_states, width = magnetic_potential_input.shape
    states = local_states * row_count
    leaf = adjacent_dense_blocks.shape[1]
    rank = distant_row_factors.shape[2]
    cluster_extent = width // leaf
    row_span = cluster_extent * col_count // row_count
    window = 0
    for target in range(row_count):
        base_t = target * row_span - target * col_count // row_count * cluster_extent
        low_t = max(base_t - REACH, 0)
        high_t = min(base_t + row_span + REACH, cluster_extent)
        window = max(window, high_t - low_t)
    block_entries = 4 * BL

    mine, stacked = reorder(magnetic_potential_input, node_reordering, col_count)

    every_block = lax.all_to_all(stacked, "col", 0, 0, tiled=True)
    pieces = []
    for target in range(row_count):
        home_t = target * col_count // row_count
        start_t = min(max(target * row_span - home_t * cluster_extent - REACH, 0), cluster_extent - window)
        pieces.append(every_block[home_t, :, start_t * leaf:(start_t + window) * leaf])
    send = jnp.concatenate(pieces, axis=0)

    ordered = lax.all_gather(mine, "row", axis=0, tiled=True)
    leaf_clusters = ordered.reshape(states, cluster_extent, leaf)
    near_window = lax.all_to_all(send, "row", 0, 0, tiled=True).reshape(states, window, leaf)

    home = row_index * col_count // row_count
    start = jnp.clip(row_index * row_span - home * cluster_extent - REACH, 0, cluster_extent - window)
    near_cols = adjacent_cluster_pairs[:, 1] - home * cluster_extent - start
    near_rows = adjacent_cluster_pairs[:, 0] - row_index * row_span
    pick = (near_cols[:, None] == jnp.arange(window, dtype=jnp.int32)[None, :]).astype(near_window.dtype)
    near_src = jnp.einsum("nw,swk->snk", pick, near_window, preferred_element_type=jnp.float32).astype(
        near_window.dtype
    )
    near_out = jnp.einsum(
        "snk,nlk->nsl", near_src, adjacent_dense_blocks, preferred_element_type=jnp.float32
    )

    v_pick = (
        (distant_column_factor_index[:, 0] - col_index * cluster_extent)[:, None]
        == jnp.arange(cluster_extent, dtype=jnp.int32)[None, :]
    ).astype(leaf_clusters.dtype)
    v_src = jnp.einsum("pc,sck->spk", v_pick, leaf_clusters, preferred_element_type=jnp.float32).astype(
        leaf_clusters.dtype
    )
    coeffs = jnp.einsum(
        "spk,pkr->psr", v_src, distant_column_factors, preferred_element_type=jnp.float32
    )
    fragments = coeffs.shape[0]
    column_indicator = (
        distant_column_factor_index[:, 1][None, :]
        == jnp.arange(block_entries, dtype=jnp.int32)[:, None]
    ).astype(jnp.float32)
    summed = jnp.dot(
        column_indicator,
        coeffs.reshape(fragments, states * rank),
        precision=lax.Precision.HIGHEST,
    ).astype(jnp.bfloat16).reshape(block_entries, states, rank)
    picked = jnp.take(summed, distant_row_factor_index[:, 1], axis=0)
    far_out = jnp.einsum(
        "psr,plr->psl", picked, distant_row_factors, preferred_element_type=jnp.float32
    )

    all_out = jnp.concatenate([near_out, far_out], axis=0)
    all_rows = jnp.concatenate([near_rows, distant_row_factor_index[:, 0] - row_index * row_span])
    scatter = (
        all_rows[None, :] == jnp.arange(row_span, dtype=jnp.int32)[:, None]
    ).astype(jnp.float32)
    partial_sum = jnp.dot(
        scatter,
        all_out.reshape(all_out.shape[0], states * leaf),
        precision=lax.Precision.HIGH,
    ).reshape(row_span, states, leaf)
    partial_sum = partial_sum.transpose(1, 0, 2).reshape(states, row_span * leaf)

    exchanged = lax.all_to_all(partial_sum, "col", 0, 0, tiled=True)
    return exchanged.reshape(col_count, states // col_count, row_span * leaf).sum(axis=0)


def solution(mesh):
    placed = (
        P("row", "col"),
        P("col"),
        P(("row", "col"), None, None),
        P(("row", "col"), None),
        P(("row", "col"), None, None),
        P(("row", "col"), None),
        P(("row", "col"), None, None),
        P(("row", "col"), None),
    )
    return jax.shard_map(
        per_device, mesh=mesh, in_specs=placed, out_specs=P("col", "row"), check_vma=False
    )
```

```python
import jax
import jax.numpy as jnp
from jax import lax
from jax.experimental import pallas as pl
from jax.experimental.pallas import tpu as pltpu
from jax.sharding import PartitionSpec as P

BL = 2
REACH = 3
LANES = 128
SUBLANES = 8
BATCH = 16


def _lane_gather_kernel(values_ref, order_ref, out_ref, copies_ref):
    rows, width = values_ref.shape
    group = SUBLANES // rows
    tiles = width // LANES
    groups = tiles // group
    batch = min(BATCH, groups)
    sub = lax.broadcasted_iota(jnp.int32, (SUBLANES, LANES), 0) // rows

    def group_body(k, carry):
        base = k * batch
        lows, highs = [], []
        for b in range(batch):
            first = (base + b) * group
            index = jnp.broadcast_to(order_ref[pl.ds(first, 1), :], (SUBLANES, LANES))
            for g in range(1, group):
                index = jnp.where(
                    sub == g, jnp.broadcast_to(order_ref[pl.ds(first + g, 1), :], (SUBLANES, LANES)), index
                )
            index = index % width
            lows.append(index % LANES)
            highs.append(index // LANES)

        def tile_body(v, accs):
            tile = values_ref[:, pl.ds(pl.multiple_of(v * LANES, LANES), LANES)].astype(jnp.float32)
            src = jnp.concatenate([tile] * group, axis=0)
            return tuple(
                jnp.where(
                    highs[b] == v,
                    jnp.take_along_axis(src, lows[b], axis=1, mode="promise_in_bounds"),
                    accs[b],
                )
                for b in range(batch)
            )

        zeros = tuple(jnp.zeros((SUBLANES, LANES), jnp.float32) for _ in range(batch))
        accs = lax.fori_loop(0, tiles, tile_body, zeros, unroll=True)
        for b in range(batch):
            for g in range(group):
                column = pl.multiple_of(((base + b) * group + g) * LANES, LANES)
                piece = accs[b][g * rows:(g + 1) * rows, :].astype(out_ref.dtype)
                out_ref[:, pl.ds(column, LANES)] = piece
                for c in range(copies_ref.shape[0]):
                    copies_ref[c, :, pl.ds(column, LANES)] = piece
        return carry

    lax.fori_loop(0, groups // batch, group_body, 0)


def reorder(values, order, copies):
    rows, width = values.shape
    return pl.pallas_call(
        _lane_gather_kernel,
        out_shape=(
            jax.ShapeDtypeStruct((rows, width), values.dtype),
            jax.ShapeDtypeStruct((copies, rows, width), values.dtype),
        ),
    )(values, order.reshape(width // LANES, LANES))


def per_device(
    magnetic_potential_input,
    node_reordering,
    adjacent_dense_blocks,
    adjacent_cluster_pairs,
    distant_row_factors,
    distant_row_factor_index,
    distant_column_factors,
    distant_column_factor_index,
):
    row_count = lax.axis_size("row")
    col_count = lax.axis_size("col")
    row_index = lax.axis_index("row")
    col_index = lax.axis_index("col")
    local_states, width = magnetic_potential_input.shape
    states = local_states * row_count
    leaf = adjacent_dense_blocks.shape[1]
    rank = distant_row_factors.shape[2]
    cluster_extent = width // leaf
    row_span = cluster_extent * col_count // row_count
    window = 0
    for target in range(row_count):
        base_t = target * row_span - target * col_count // row_count * cluster_extent
        low_t = max(base_t - REACH, 0)
        high_t = min(base_t + row_span + REACH, cluster_extent)
        window = max(window, high_t - low_t)
    block_entries = 4 * BL

    mine, stacked = reorder(magnetic_potential_input, node_reordering, col_count)

    every_block = lax.all_to_all(stacked, "col", 0, 0, tiled=True)
    pieces = []
    for target in range(row_count):
        home_t = target * col_count // row_count
        start_t = min(max(target * row_span - home_t * cluster_extent - REACH, 0), cluster_extent - window)
        pieces.append(every_block[home_t, :, start_t * leaf:(start_t + window) * leaf])
    send = jnp.concatenate(pieces, axis=0)

    ordered = lax.all_gather(mine, "row", axis=0, tiled=True)
    leaf_clusters = ordered.reshape(states, cluster_extent, leaf)
    near_window = lax.all_to_all(send, "row", 0, 0, tiled=True).reshape(states, window, leaf)

    home = row_index * col_count // row_count
    start = jnp.clip(row_index * row_span - home * cluster_extent - REACH, 0, cluster_extent - window)
    near_cols = adjacent_cluster_pairs[:, 1] - home * cluster_extent - start
    near_rows = adjacent_cluster_pairs[:, 0] - row_index * row_span
    pick = (near_cols[:, None] == jnp.arange(window, dtype=jnp.int32)[None, :]).astype(near_window.dtype)
    near_src = jnp.einsum("nw,swk->snk", pick, near_window, preferred_element_type=jnp.float32).astype(
        near_window.dtype
    )
    near_out = jnp.einsum(
        "snk,nlk->nsl", near_src, adjacent_dense_blocks, preferred_element_type=jnp.float32
    )

    v_pick = (
        (distant_column_factor_index[:, 0] - col_index * cluster_extent)[:, None]
        == jnp.arange(cluster_extent, dtype=jnp.int32)[None, :]
    ).astype(leaf_clusters.dtype)
    v_src = jnp.einsum("pc,sck->psk", v_pick, leaf_clusters, preferred_element_type=jnp.float32).astype(
        leaf_clusters.dtype
    )
    coeffs = jnp.einsum(
        "psk,pkr->psr", v_src, distant_column_factors, preferred_element_type=jnp.float32
    )
    fragments = coeffs.shape[0]
    column_indicator = (
        distant_column_factor_index[:, 1][None, :]
        == jnp.arange(block_entries, dtype=jnp.int32)[:, None]
    ).astype(jnp.float32)
    summed = jnp.dot(
        column_indicator,
        coeffs.reshape(fragments, states * rank),
        precision=lax.Precision.HIGHEST,
    ).astype(jnp.bfloat16).reshape(block_entries, states, rank)
    picked = jnp.take(summed, distant_row_factor_index[:, 1], axis=0)
    far_out = jnp.einsum(
        "psr,plr->psl", picked, distant_row_factors, preferred_element_type=jnp.float32
    )

    all_out = jnp.concatenate([near_out, far_out], axis=0)
    all_rows = jnp.concatenate([near_rows, distant_row_factor_index[:, 0] - row_index * row_span])
    scatter = (
        all_rows[None, :] == jnp.arange(row_span, dtype=jnp.int32)[:, None]
    ).astype(jnp.float32)
    partial_sum = jnp.dot(
        scatter,
        all_out.reshape(all_out.shape[0], states * leaf),
        precision=lax.Precision.HIGH,
    ).reshape(row_span, states, leaf)
    partial_sum = partial_sum.transpose(1, 0, 2).reshape(states, row_span * leaf)

    exchanged = lax.all_to_all(partial_sum, "col", 0, 0, tiled=True)
    return exchanged.reshape(col_count, states // col_count, row_span * leaf).sum(axis=0)


def solution(mesh):
    placed = (
        P("row", "col"),
        P("col"),
        P(("row", "col"), None, None),
        P(("row", "col"), None),
        P(("row", "col"), None, None),
        P(("row", "col"), None),
        P(("row", "col"), None, None),
        P(("row", "col"), None),
    )
    return jax.shard_map(
        per_device, mesh=mesh, in_specs=placed, out_specs=P("col", "row"), check_vma=False
    )
```

```python
import jax
import jax.numpy as jnp
from jax import lax
from jax.experimental import pallas as pl
from jax.experimental.pallas import tpu as pltpu
from jax.sharding import PartitionSpec as P

BL = 2
REACH = 3
LANES = 128
SUBLANES = 8
BATCH = 16


def _lane_gather_kernel(values_ref, order_ref, out_ref, copies_ref):
    rows, width = values_ref.shape
    group = SUBLANES // rows
    tiles = width // LANES
    groups = tiles // group
    batch = min(BATCH, groups)
    sub = lax.broadcasted_iota(jnp.int32, (SUBLANES, LANES), 0) // rows

    def group_body(k, carry):
        base = k * batch
        lows, highs = [], []
        for b in range(batch):
            first = (base + b) * group
            index = jnp.broadcast_to(order_ref[pl.ds(first, 1), :], (SUBLANES, LANES))
            for g in range(1, group):
                index = jnp.where(
                    sub == g, jnp.broadcast_to(order_ref[pl.ds(first + g, 1), :], (SUBLANES, LANES)), index
                )
            index = index % width
            lows.append(index % LANES)
            highs.append(index // LANES)

        def tile_body(v, accs):
            tile = values_ref[:, pl.ds(pl.multiple_of(v * LANES, LANES), LANES)].astype(jnp.float32)
            src = jnp.concatenate([tile] * group, axis=0)
            return tuple(
                jnp.where(
                    highs[b] == v,
                    jnp.take_along_axis(src, lows[b], axis=1, mode="promise_in_bounds"),
                    accs[b],
                )
                for b in range(batch)
            )

        zeros = tuple(jnp.zeros((SUBLANES, LANES), jnp.float32) for _ in range(batch))
        accs = lax.fori_loop(0, tiles, tile_body, zeros, unroll=True)
        for b in range(batch):
            for g in range(group):
                column = pl.multiple_of(((base + b) * group + g) * LANES, LANES)
                piece = accs[b][g * rows:(g + 1) * rows, :].astype(out_ref.dtype)
                out_ref[:, pl.ds(column, LANES)] = piece
                for c in range(copies_ref.shape[0]):
                    copies_ref[c, :, pl.ds(column, LANES)] = piece
        return carry

    lax.fori_loop(0, groups // batch, group_body, 0)


def reorder(values, order, copies):
    rows, width = values.shape
    return pl.pallas_call(
        _lane_gather_kernel,
        out_shape=(
            jax.ShapeDtypeStruct((rows, width), values.dtype),
            jax.ShapeDtypeStruct((copies, rows, width), values.dtype),
        ),
    )(values, order.reshape(width // LANES, LANES))


def per_device(
    magnetic_potential_input,
    node_reordering,
    adjacent_dense_blocks,
    adjacent_cluster_pairs,
    distant_row_factors,
    distant_row_factor_index,
    distant_column_factors,
    distant_column_factor_index,
):
    row_count = lax.axis_size("row")
    col_count = lax.axis_size("col")
    row_index = lax.axis_index("row")
    col_index = lax.axis_index("col")
    local_states, width = magnetic_potential_input.shape
    states = local_states * row_count
    leaf = adjacent_dense_blocks.shape[1]
    rank = distant_row_factors.shape[2]
    cluster_extent = width // leaf
    row_span = cluster_extent * col_count // row_count
    window = 0
    for target in range(row_count):
        base_t = target * row_span - target * col_count // row_count * cluster_extent
        low_t = max(base_t - REACH, 0)
        high_t = min(base_t + row_span + REACH, cluster_extent)
        window = max(window, high_t - low_t)
    block_entries = 4 * BL

    mine, stacked = reorder(magnetic_potential_input, node_reordering, col_count)

    every_block = lax.all_to_all(stacked, "col", 0, 0, tiled=True)
    pieces = []
    for target in range(row_count):
        home_t = target * col_count // row_count
        start_t = min(max(target * row_span - home_t * cluster_extent - REACH, 0), cluster_extent - window)
        pieces.append(every_block[home_t, :, start_t * leaf:(start_t + window) * leaf])
    send = jnp.concatenate(pieces, axis=0)

    ordered = lax.all_gather(mine, "row", axis=0, tiled=True)
    leaf_clusters = ordered.reshape(states, cluster_extent, leaf)
    near_window = lax.all_to_all(send, "row", 0, 0, tiled=True).reshape(states, window, leaf)

    home = row_index * col_count // row_count
    start = jnp.clip(row_index * row_span - home * cluster_extent - REACH, 0, cluster_extent - window)
    near_cols = adjacent_cluster_pairs[:, 1] - home * cluster_extent - start
    near_rows = adjacent_cluster_pairs[:, 0] - row_index * row_span
    pick = (near_cols[:, None] == jnp.arange(window, dtype=jnp.int32)[None, :]).astype(near_window.dtype)
    near_src = jnp.einsum("nw,swk->nsk", pick, near_window, preferred_element_type=jnp.float32).astype(
        near_window.dtype
    )
    near_out = jnp.einsum(
        "nsk,nlk->nsl", near_src, adjacent_dense_blocks, preferred_element_type=jnp.float32
    )

    v_pick = (
        (distant_column_factor_index[:, 0] - col_index * cluster_extent)[:, None]
        == jnp.arange(cluster_extent, dtype=jnp.int32)[None, :]
    ).astype(leaf_clusters.dtype)
    v_src = jnp.einsum("pc,sck->spk", v_pick, leaf_clusters, preferred_element_type=jnp.float32).astype(
        leaf_clusters.dtype
    )
    coeffs = jnp.einsum(
        "spk,pkr->psr", v_src, distant_column_factors, preferred_element_type=jnp.float32
    )
    fragments = coeffs.shape[0]
    column_indicator = (
        distant_column_factor_index[:, 1][None, :]
        == jnp.arange(block_entries, dtype=jnp.int32)[:, None]
    ).astype(jnp.float32)
    summed = jnp.dot(
        column_indicator,
        coeffs.reshape(fragments, states * rank),
        precision=lax.Precision.HIGHEST,
    ).astype(jnp.bfloat16).reshape(block_entries, states, rank)
    picked = jnp.take(summed, distant_row_factor_index[:, 1], axis=0)
    far_out = jnp.einsum(
        "psr,plr->psl", picked, distant_row_factors, preferred_element_type=jnp.float32
    )

    all_out = jnp.concatenate([near_out, far_out], axis=0)
    all_rows = jnp.concatenate([near_rows, distant_row_factor_index[:, 0] - row_index * row_span])
    scatter = (
        all_rows[None, :] == jnp.arange(row_span, dtype=jnp.int32)[:, None]
    ).astype(jnp.float32)
    partial_sum = jnp.dot(
        scatter,
        all_out.reshape(all_out.shape[0], states * leaf),
        precision=lax.Precision.HIGH,
    ).reshape(row_span, states, leaf)
    partial_sum = partial_sum.transpose(1, 0, 2).reshape(states, row_span * leaf)

    exchanged = lax.all_to_all(partial_sum, "col", 0, 0, tiled=True)
    return exchanged.reshape(col_count, states // col_count, row_span * leaf).sum(axis=0)


def solution(mesh):
    placed = (
        P("row", "col"),
        P("col"),
        P(("row", "col"), None, None),
        P(("row", "col"), None),
        P(("row", "col"), None, None),
        P(("row", "col"), None),
        P(("row", "col"), None, None),
        P(("row", "col"), None),
    )
    return jax.shard_map(
        per_device, mesh=mesh, in_specs=placed, out_specs=P("col", "row"), check_vma=False
    )
```

```python
import jax
import jax.numpy as jnp
from jax import lax
from jax.experimental import pallas as pl
from jax.experimental.pallas import tpu as pltpu
from jax.sharding import PartitionSpec as P

BL = 2
REACH = 3
LANES = 128
SUBLANES = 8
BATCH = 32


def _lane_gather_kernel(values_ref, order_ref, out_ref, copies_ref):
    rows, width = values_ref.shape
    group = SUBLANES // rows
    tiles = width // LANES
    groups = tiles // group
    batch = min(BATCH, groups)
    sub = lax.broadcasted_iota(jnp.int32, (SUBLANES, LANES), 0) // rows

    def group_body(k, carry):
        base = k * batch
        lows, highs = [], []
        for b in range(batch):
            first = (base + b) * group
            index = jnp.broadcast_to(order_ref[pl.ds(first, 1), :], (SUBLANES, LANES))
            for g in range(1, group):
                index = jnp.where(
                    sub == g, jnp.broadcast_to(order_ref[pl.ds(first + g, 1), :], (SUBLANES, LANES)), index
                )
            index = index % width
            lows.append(index % LANES)
            highs.append(index // LANES)

        def tile_body(v, accs):
            tile = values_ref[:, pl.ds(pl.multiple_of(v * LANES, LANES), LANES)].astype(jnp.float32)
            src = jnp.concatenate([tile] * group, axis=0)
            return tuple(
                jnp.where(
                    highs[b] == v,
                    jnp.take_along_axis(src, lows[b], axis=1, mode="promise_in_bounds"),
                    accs[b],
                )
                for b in range(batch)
            )

        zeros = tuple(jnp.zeros((SUBLANES, LANES), jnp.float32) for _ in range(batch))
        accs = lax.fori_loop(0, tiles, tile_body, zeros, unroll=True)
        for b in range(batch):
            for g in range(group):
                column = pl.multiple_of(((base + b) * group + g) * LANES, LANES)
                piece = accs[b][g * rows:(g + 1) * rows, :].astype(out_ref.dtype)
                out_ref[:, pl.ds(column, LANES)] = piece
                for c in range(copies_ref.shape[0]):
                    copies_ref[c, :, pl.ds(column, LANES)] = piece
        return carry

    lax.fori_loop(0, groups // batch, group_body, 0)


def reorder(values, order, copies):
    rows, width = values.shape
    return pl.pallas_call(
        _lane_gather_kernel,
        out_shape=(
            jax.ShapeDtypeStruct((rows, width), values.dtype),
            jax.ShapeDtypeStruct((copies, rows, width), values.dtype),
        ),
    )(values, order.reshape(width // LANES, LANES))


def per_device(
    magnetic_potential_input,
    node_reordering,
    adjacent_dense_blocks,
    adjacent_cluster_pairs,
    distant_row_factors,
    distant_row_factor_index,
    distant_column_factors,
    distant_column_factor_index,
):
    row_count = lax.axis_size("row")
    col_count = lax.axis_size("col")
    row_index = lax.axis_index("row")
    col_index = lax.axis_index("col")
    local_states, width = magnetic_potential_input.shape
    states = local_states * row_count
    leaf = adjacent_dense_blocks.shape[1]
    rank = distant_row_factors.shape[2]
    cluster_extent = width // leaf
    row_span = cluster_extent * col_count // row_count
    window = 0
    for target in range(row_count):
        base_t = target * row_span - target * col_count // row_count * cluster_extent
        low_t = max(base_t - REACH, 0)
        high_t = min(base_t + row_span + REACH, cluster_extent)
        window = max(window, high_t - low_t)
    block_entries = 4 * BL

    mine, stacked = reorder(magnetic_potential_input, node_reordering, col_count)

    every_block = lax.all_to_all(stacked, "col", 0, 0, tiled=True)
    pieces = []
    for target in range(row_count):
        home_t = target * col_count // row_count
        start_t = min(max(target * row_span - home_t * cluster_extent - REACH, 0), cluster_extent - window)
        pieces.append(every_block[home_t, :, start_t * leaf:(start_t + window) * leaf])
    send = jnp.concatenate(pieces, axis=0)

    ordered = lax.all_gather(mine, "row", axis=0, tiled=True)
    leaf_clusters = ordered.reshape(states, cluster_extent, leaf)
    near_window = lax.all_to_all(send, "row", 0, 0, tiled=True).reshape(states, window, leaf)

    home = row_index * col_count // row_count
    start = jnp.clip(row_index * row_span - home * cluster_extent - REACH, 0, cluster_extent - window)
    near_cols = adjacent_cluster_pairs[:, 1] - home * cluster_extent - start
    near_rows = adjacent_cluster_pairs[:, 0] - row_index * row_span
    pick = (near_cols[:, None] == jnp.arange(window, dtype=jnp.int32)[None, :]).astype(near_window.dtype)
    near_src = jnp.einsum("nw,swk->snk", pick, near_window, preferred_element_type=jnp.float32).astype(
        near_window.dtype
    )
    near_out = jnp.einsum(
        "snk,nlk->nsl", near_src, adjacent_dense_blocks, preferred_element_type=jnp.float32
    )

    v_pick = (
        (distant_column_factor_index[:, 0] - col_index * cluster_extent)[:, None]
        == jnp.arange(cluster_extent, dtype=jnp.int32)[None, :]
    ).astype(leaf_clusters.dtype)
    v_src = jnp.einsum("pc,sck->spk", v_pick, leaf_clusters, preferred_element_type=jnp.float32).astype(
        leaf_clusters.dtype
    )
    coeffs = jnp.einsum(
        "spk,pkr->psr", v_src, distant_column_factors, preferred_element_type=jnp.float32
    )
    fragments = coeffs.shape[0]
    column_indicator = (
        distant_column_factor_index[:, 1][None, :]
        == jnp.arange(block_entries, dtype=jnp.int32)[:, None]
    ).astype(jnp.float32)
    summed = jnp.dot(
        column_indicator,
        coeffs.reshape(fragments, states * rank),
        precision=lax.Precision.HIGHEST,
    ).astype(jnp.bfloat16).reshape(block_entries, states, rank)
    picked = jnp.take(summed, distant_row_factor_index[:, 1], axis=0)
    far_out = jnp.einsum(
        "psr,plr->psl", picked, distant_row_factors, preferred_element_type=jnp.float32
    )

    all_out = jnp.concatenate([near_out, far_out], axis=0)
    all_rows = jnp.concatenate([near_rows, distant_row_factor_index[:, 0] - row_index * row_span])
    scatter = (
        all_rows[None, :] == jnp.arange(row_span, dtype=jnp.int32)[:, None]
    ).astype(jnp.float32)
    partial_sum = jnp.dot(
        scatter,
        all_out.reshape(all_out.shape[0], states * leaf),
        precision=lax.Precision.HIGH,
    ).reshape(row_span, states, leaf)
    partial_sum = partial_sum.transpose(1, 0, 2).reshape(states, row_span * leaf)

    exchanged = lax.all_to_all(partial_sum, "col", 0, 0, tiled=True)
    return exchanged.reshape(col_count, states // col_count, row_span * leaf).sum(axis=0)


def solution(mesh):
    placed = (
        P("row", "col"),
        P("col"),
        P(("row", "col"), None, None),
        P(("row", "col"), None),
        P(("row", "col"), None, None),
        P(("row", "col"), None),
        P(("row", "col"), None, None),
        P(("row", "col"), None),
    )
    return jax.shard_map(
        per_device, mesh=mesh, in_specs=placed, out_specs=P("col", "row"), check_vma=False
    )
```
